32 devices in a mesh: groups: 2 (over x), sy: 16 (over z, y, core).
Axes of the slice: x: 2, y: 2, z: 4, core: 2. Of those that a mesh axis runs over, the one named last changes fastest.
Arguments:
- queries: bfloat16 [64, 64, 2, 1536], P('sy', 'groups'), parts along dimension 1, may hold values from -6 to 6
- key_vecs: bfloat16 [64, 64, 2, 1536], P('sy', 'groups'), parts along dimension 1, may hold values from -6 to 6
- value_vecs: bfloat16 [64, 64, 2, 1536], P('sy', 'groups'), parts along dimension 1, may hold values from -6 to 6
- outputs_fwd: bfloat16 [64, 64, 2, 1536], P('sy', 'groups'), parts along dimension 1, may hold values from -1.5 to 1.5
- grad_out: bfloat16 [64, 64, 2, 1536], P('sy', 'groups'), parts along dimension 1, may hold values from -96 to 96
- log_norm: float32 [64, 64, 2, 12], P('sy', 'groups'), parts along dimension 1, may hold values from 6.5 to 8.5
Outputs:
- grad_queries: bfloat16 [64, 64, 2, 1536], P('sy', 'groups'), parts along dimension 1
- grad_keys: bfloat16 [64, 64, 2, 1536], P('sy', 'groups'), parts along dimension 1
- grad_values: bfloat16 [64, 64, 2, 1536], P('sy', 'groups'), parts along dimension 1
The draws below stay inside these ranges and needn't reach their ends.
There are 2 independent parts, one for each index of `groups`. The reference program is written for one: setup_inputs(seed, part) draws one part's arguments, and reference() takes and returns one part's arrays. A program takes and returns all parts, laid end to end along the dimension named above; each array names one. Nothing has to cross between parts.
All inputs are finite; a program needn't handle non-finite values.
Results may differ from the reference program's by a relative error of at most 0.0057.
Values may be sent and summed in bfloat16 or wider, within the bound.
No kernel may reach another device: no remote copies, remote signals or barrier semaphores. Data moves between devices by JAX's collectives and lax.ppermute only.
A program may use at most 128 MiB of HBM per device.

```python
import jax
import jax.numpy as jnp
from jax import lax

HEADS = 12
WIDTH = 32
FRAMES = 2
HEIGHT = 64
CHANNELS = 1536


def shard_levels(rng, shape, shards, low, largest):
    def one(position, parts):
        steps = jax.random.uniform(jax.random.fold_in(jax.random.fold_in(rng, 6), position), (parts,), jnp.float32, low / len(shards), largest / len(shards))
        return jnp.repeat(jnp.exp(steps), shape[position] // parts).reshape((-1,) + (1,) * (len(shape) - position - 1))

    factor_of = one(*shards[0])
    for cut in shards[1:]:
        factor_of = factor_of * one(*cut)
    return factor_of


def centred(stream_key, dims, deviation, limit, cuts=(), kind=jnp.bfloat16):
    result = deviation * jax.random.normal(stream_key, dims, jnp.float32)
    if cuts:
        result = result * shard_levels(stream_key, dims, cuts, -0.22, 0.18)
    return jnp.clip(result, -limit, limit).astype(kind)


def setup_inputs(seed: int = 0, part: int = 0) -> dict:
    streams_of = jax.random.split(jax.random.key(seed), 7)
    part_splits = jax.random.split(jax.random.fold_in(streams_of[6], part), 7)
    return {
        "queries": centred(part_splits[0], (HEIGHT, WIDTH, FRAMES, CHANNELS), 1.0, 6.0, ((0, 16),)),
        "key_vecs": centred(part_splits[1], (HEIGHT, WIDTH, FRAMES, CHANNELS), 1.0, 6.0, ((0, 16),)),
        "value_vecs": centred(part_splits[2], (HEIGHT, WIDTH, FRAMES, CHANNELS), 1.0, 6.0, ((0, 16),)),
        "outputs_fwd": centred(part_splits[3], (HEIGHT, WIDTH, FRAMES, CHANNELS), 0.25, 1.5, ((0, 16),)),
        "grad_out": centred(part_splits[4], (HEIGHT, WIDTH, FRAMES, CHANNELS), 16.0, 96.0, ((0, 16),)),
        "log_norm": jnp.clip(6.5 + 2.0 * jax.random.uniform(part_splits[5], (HEIGHT, WIDTH, FRAMES, HEADS), jnp.float32) ** shard_levels(part_splits[5], (HEIGHT, WIDTH, FRAMES, HEADS), ((0, 16),), -0.2, 0.2), 6.5, 8.5),
    }


def reference(queries, key_vecs, value_vecs, outputs_fwd, grad_out, log_norm):
    height, width_cells, frames, channels = queries.shape
    head_dim = channels // HEADS
    scaling = head_dim ** -0.5
    tiles_w = width_cells // 8
    row_delta = jnp.sum((grad_out.astype(jnp.float32) * outputs_fwd.astype(jnp.float32)).reshape(height, width_cells, frames, HEADS, head_dim), axis=-1)
    column_index = (8 * jnp.arange(tiles_w, dtype=jnp.int32)[:, None] - 4 + jnp.arange(16, dtype=jnp.int32)[None, :]) % width_cells

    def query_heads(array):
        array = array.astype(jnp.float32).reshape(8, tiles_w, 8, frames, HEADS, head_dim)
        return jnp.transpose(array, (1, 4, 0, 2, 3, 5)).reshape(tiles_w, HEADS, 64 * frames, head_dim)

    def query_stats(array):
        array = array.reshape(8, tiles_w, 8, frames, HEADS)
        return jnp.transpose(array, (1, 4, 0, 2, 3)).reshape(tiles_w, HEADS, 64 * frames)

    def key_heads(array):
        array = array[:, column_index].astype(jnp.float32).reshape(16, tiles_w, 16, frames, HEADS, head_dim)
        return jnp.transpose(array, (1, 4, 0, 2, 3, 5)).reshape(tiles_w, HEADS, 256 * frames, head_dim)

    def back_keys(array):
        array = jnp.transpose(array.reshape(tiles_w, HEADS, 16, 16, frames, head_dim), (2, 0, 3, 4, 1, 5))
        return array.reshape(16, tiles_w, 16, frames, channels)

    def tile_step(totals, tile_row):
        total_keys, total_values = totals
        query_rows = tile_row * 8 + jnp.arange(8, dtype=jnp.int32)
        key_rows = (tile_row * 8 - 4 + jnp.arange(16, dtype=jnp.int32)) % height
        query_head = query_heads(queries[query_rows])
        dout_head = query_heads(grad_out[query_rows])
        norm_head = query_stats(log_norm[query_rows])
        delta_head = query_stats(row_delta[query_rows])
        key_head = key_heads(key_vecs[key_rows])
        value_head = key_heads(value_vecs[key_rows])
        scores = jnp.einsum('bhqd,bhkd->bhqk', query_head, key_head) * scaling
        attention = jnp.exp(scores - norm_head[..., None])
        grad_attention = jnp.einsum('bhqd,bhkd->bhqk', dout_head, value_head)
        grad_scores = lax.optimization_barrier((attention * (grad_attention - delta_head[..., None])).astype(jnp.bfloat16)).astype(jnp.float32)
        attention_b = lax.optimization_barrier(attention.astype(jnp.bfloat16)).astype(jnp.float32)
        grad_q = jnp.einsum('bhqk,bhkd->bhqd', grad_scores, key_head) * scaling
        grad_k = jnp.einsum('bhqk,bhqd->bhkd', grad_scores, query_head) * scaling
        grad_v = jnp.einsum('bhqk,bhqd->bhkd', attention_b, dout_head)
        grad_q = jnp.transpose(grad_q.reshape(tiles_w, HEADS, 8, 8, frames, head_dim), (2, 0, 3, 4, 1, 5)).reshape(8, width_cells, frames, channels)
        total_keys = total_keys.at[key_rows[:, None, None], column_index[None, :, :]].add(back_keys(grad_k))
        total_values = total_values.at[key_rows[:, None, None], column_index[None, :, :]].add(back_keys(grad_v))
        return (total_keys, total_values), grad_q.astype(jnp.bfloat16)

    zero_grid = jnp.zeros((height, width_cells, frames, channels), jnp.float32)
    (total_keys, total_values), query_tiles = lax.scan(tile_step, (zero_grid, zero_grid), jnp.arange(height // 8, dtype=jnp.int32))
    grad_queries = query_tiles.reshape(height, width_cells, frames, channels)
    return grad_queries, total_keys.astype(jnp.bfloat16), total_values.astype(jnp.bfloat16)
```

```python
import functools

import jax
import jax.numpy as jnp
from jax import lax
from jax.experimental import pallas as pl
from jax.experimental.pallas import tpu as pltpu
from jax.sharding import PartitionSpec as P

HEAD_DIM = 128
TILE = 8
MARGIN = 4


def swap(block, pairs_of):
    n = lax.axis_size("sy")
    route = []
    for i in range(n):
        route.append((i, pairs_of(i, n)))
    return lax.ppermute(block, "sy", route)


def core_partner(i, n):
    return i ^ 1


def chip_neighbour(i, n):
    return (i + 1) % n if i % 2 else (i - 1) % n


def window_kernel(q_ref, do_ref, lse_ref, delta_ref, k_ref, v_ref, dq_ref, dk_ref, dv_ref, *, tiles, tf, mf):
    scaling = HEAD_DIM ** (-0.5)
    rows = q_ref.shape[0]
    krows = k_ref.shape[0]
    width = dk_ref.shape[1]
    span = tf + 2 * mf
    dk_ref[...] = jnp.zeros_like(dk_ref)
    dv_ref[...] = jnp.zeros_like(dv_ref)
    for b in range(tiles):
        kw = k_ref[:, b * tf : b * tf + span, :].reshape(krows * span, HEAD_DIM)
        vw = v_ref[:, b * tf : b * tf + span, :].reshape(krows * span, HEAD_DIM)
        qb = q_ref[:, b * tf : (b + 1) * tf, :].reshape(rows * tf, HEAD_DIM)
        dob = do_ref[:, b * tf : (b + 1) * tf, :].reshape(rows * tf, HEAD_DIM)
        nt = (((1,), (1,)), ((), ()))
        scores = lax.dot_general(kw, qb, nt, preferred_element_type=jnp.float32) * scaling
        attention = jnp.exp(scores - lse_ref[b])
        grad_attention = lax.dot_general(vw, dob, nt, preferred_element_type=jnp.float32)
        grad_scores = (attention * (grad_attention - delta_ref[b])).astype(jnp.bfloat16)
        grad_v = jnp.dot(attention.astype(jnp.bfloat16), dob, preferred_element_type=jnp.float32)
        grad_k = jnp.dot(grad_scores, qb, preferred_element_type=jnp.float32) * scaling
        grad_q = (
            jnp.dot(grad_scores.T, kw, preferred_element_type=jnp.float32) * scaling
        )
        dq_ref[:, b * tf : (b + 1) * tf, :] = grad_q.reshape(rows, tf, HEAD_DIM).astype(dq_ref.dtype)
        grad_k = grad_k.reshape(krows, span, HEAD_DIM)
        grad_v = grad_v.reshape(krows, span, HEAD_DIM)
        start = b * tf - mf
        pieces = []
        if start < 0:
            pieces.append((0, width + start, -start))
            pieces.append((-start, 0, span + start))
        elif start + span > width:
            pieces.append((0, start, width - start))
            pieces.append((width - start, 0, start + span - width))
        else:
            pieces.append((0, start, span))
        for src, dst, size in pieces:
            dk_ref[:, dst : dst + size, :] += grad_k[:, src : src + size, :]
            dv_ref[:, dst : dst + size, :] += grad_v[:, src : src + size, :]


def window_pass(q, do, lse_t, delta_t, k_ext, v_ext, tiles, tf, mf):
    rows, width, channels = q.shape
    krows = k_ext.shape[0]
    ext = k_ext.shape[1]
    heads = channels // HEAD_DIM
    kernel = functools.partial(window_kernel, tiles=tiles, tf=tf, mf=mf)
    qspec = pl.BlockSpec((rows, width, HEAD_DIM), lambda h: (0, 0, h))
    kspec = pl.BlockSpec((krows, ext, HEAD_DIM), lambda h: (0, 0, h))
    sspec = pl.BlockSpec((None, tiles, 1, rows * tf), lambda h: (h, 0, 0, 0))
    ospec = pl.BlockSpec((krows, width, HEAD_DIM), lambda h: (0, 0, h))
    pairs = tiles * rows * tf * krows * (tf + 2 * mf) * heads
    cost = pl.CostEstimate(
        flops=10 * pairs * HEAD_DIM,
        transcendentals=pairs,
        bytes_accessed=2 * (2 * q.size + 2 * k_ext.size + q.size) + 8 * krows * width * channels,
    )
    return pl.pallas_call(
        kernel,
        grid=(heads,),
        in_specs=[qspec, qspec, sspec, sspec, kspec, kspec],
        out_specs=[qspec, ospec, ospec],
        out_shape=[
            jax.ShapeDtypeStruct((rows, width, channels), jnp.bfloat16),
            jax.ShapeDtypeStruct((krows, width, channels), jnp.float32),
            jax.ShapeDtypeStruct((krows, width, channels), jnp.float32),
        ],
        cost_estimate=cost,
    )(q, do, lse_t, delta_t, k_ext, v_ext)


def stats_tiles(stats, tiles, tf):
    rows, width, heads = stats.shape
    tiled = stats.reshape(rows, tiles, tf, heads)
    tiled = jnp.transpose(tiled, (3, 1, 0, 2))
    return tiled.reshape(heads, tiles, 1, rows * tf)


def on_device(queries, key_vecs, value_vecs, outputs_fwd, grad_out, log_norm):
    rows, width_cells, frames, channels = queries.shape
    heads = log_norm.shape[3]
    width = width_cells * frames
    tiles = width_cells // TILE
    tf = TILE * frames
    mf = MARGIN * frames

    q = queries.reshape(rows, width, channels)
    do = grad_out.reshape(rows, width, channels)
    row_delta = jnp.einsum(
        "rwhd,rwhd->rwh",
        grad_out.reshape(rows, width, heads, HEAD_DIM),
        outputs_fwd.reshape(rows, width, heads, HEAD_DIM),
        preferred_element_type=jnp.float32,
    )
    lse_t = stats_tiles(log_norm.reshape(rows, width, heads), tiles, tf)
    delta_t = stats_tiles(row_delta, tiles, tf)

    kv_own = jnp.stack([key_vecs.reshape(rows, width, channels), value_vecs.reshape(rows, width, channels)])
    kv_partner = swap(kv_own, core_partner)
    kv_cross = swap(kv_own, chip_neighbour)
    kv_forward = swap(kv_cross, core_partner)
    kv_rows = jnp.concatenate([kv_own, kv_partner, kv_cross, kv_forward], axis=1)
    kv_ext = jnp.concatenate([kv_rows[:, :, width - mf :], kv_rows, kv_rows[:, :, :mf]], axis=2)

    dq, dk, dv = window_pass(q, do, lse_t, delta_t, kv_ext[0], kv_ext[1], tiles, tf, mf)

    parts = jnp.stack([dk, dv]).reshape(2, 4, rows, width, channels)
    back = swap(parts[:, 1:4:2], core_partner)
    own_total = parts[:, 0] + back[:, 0]
    cross_total = parts[:, 2] + back[:, 1]
    arrived = swap(cross_total, chip_neighbour)
    total = own_total + arrived
    grad_keys = total[0].astype(jnp.bfloat16).reshape(rows, width_cells, frames, channels)
    grad_values = total[1].astype(jnp.bfloat16).reshape(rows, width_cells, frames, channels)
    grad_queries = dq.reshape(rows, width_cells, frames, channels)
    return (grad_queries, grad_keys, grad_values)


def solution(mesh):
    spec = P("sy", "groups", None, None)
    return jax.shard_map(
        on_device,
        mesh=mesh,
        in_specs=(spec,) * 6,
        out_specs=(spec,) * 3,
        check_vma=False,
    )
```

```python
import functools

import jax
import jax.numpy as jnp
from jax import lax
from jax.experimental import pallas as pl
from jax.experimental.pallas import tpu as pltpu
from jax.sharding import PartitionSpec as P

HEAD_DIM = 128
TILE = 8
MARGIN = 4


def swap(block, pairs_of):
    n = lax.axis_size("sy")
    route = []
    for i in range(n):
        route.append((i, pairs_of(i, n)))
    return lax.ppermute(block, "sy", route)


def core_partner(i, n):
    return i ^ 1


def chip_neighbour(i, n):
    return (i + 1) % n if i % 2 else (i - 1) % n


def window_kernel(
    q_ref, do_ref, lse_ref, delta_ref, k_ref, v_ref, dq_ref, own_ref, intra_ref, cross_ref, *, tiles, tf, mf
):
    scaling = HEAD_DIM ** (-0.5)
    rows = q_ref.shape[0]
    krows = k_ref.shape[0]
    width = own_ref.shape[2]
    span = tf + 2 * mf
    own_ref[...] = jnp.zeros_like(own_ref)
    intra_ref[...] = jnp.zeros_like(intra_ref)
    cross_ref[...] = jnp.zeros_like(cross_ref)
    targets = [own_ref, intra_ref.at[0], cross_ref, intra_ref.at[1]]
    blocks = krows // rows
    for b in range(tiles):
        kw = k_ref[:, b * tf : b * tf + span, :].reshape(krows * span, HEAD_DIM)
        vw = v_ref[:, b * tf : b * tf + span, :].reshape(krows * span, HEAD_DIM)
        qb = q_ref[:, b * tf : (b + 1) * tf, :].reshape(rows * tf, HEAD_DIM)
        dob = do_ref[:, b * tf : (b + 1) * tf, :].reshape(rows * tf, HEAD_DIM)
        nt = (((1,), (1,)), ((), ()))
        scores = lax.dot_general(kw, qb, nt, preferred_element_type=jnp.float32) * scaling
        attention = jnp.exp(scores - lse_ref[b])
        grad_attention = lax.dot_general(vw, dob, nt, preferred_element_type=jnp.float32)
        grad_scores = (attention * (grad_attention - delta_ref[b])).astype(jnp.bfloat16)
        grad_v = jnp.dot(attention.astype(jnp.bfloat16), dob, preferred_element_type=jnp.float32)
        grad_k = jnp.dot(grad_scores, qb, preferred_element_type=jnp.float32) * scaling
        grad_q = jnp.dot(grad_scores.T, kw, preferred_element_type=jnp.float32) * scaling
        dq_ref[:, b * tf : (b + 1) * tf, :] = grad_q.reshape(rows, tf, HEAD_DIM).astype(dq_ref.dtype)
        grad_k = grad_k.reshape(blocks, rows, span, HEAD_DIM)
        grad_v = grad_v.reshape(blocks, rows, span, HEAD_DIM)
        start = b * tf - mf
        pieces = []
        if start < 0:
            pieces.append((0, width + start, -start))
            pieces.append((-start, 0, span + start))
        elif start + span > width:
            pieces.append((0, start, width - start))
            pieces.append((width - start, 0, start + span - width))
        else:
            pieces.append((0, start, span))
        for block, target in enumerate(targets):
            for src, dst, size in pieces:
                target[0, :, dst : dst + size, :] += grad_k[block, :, src : src + size, :]
                target[1, :, dst : dst + size, :] += grad_v[block, :, src : src + size, :]


def window_pass(q, do, lse_t, delta_t, k_ext, v_ext, tiles, tf, mf):
    rows, width, channels = q.shape
    krows = k_ext.shape[0]
    ext = k_ext.shape[1]
    heads = channels // HEAD_DIM
    kernel = functools.partial(window_kernel, tiles=tiles, tf=tf, mf=mf)
    qspec = pl.BlockSpec((rows, width, HEAD_DIM), lambda h: (0, 0, h))
    kspec = pl.BlockSpec((krows, ext, HEAD_DIM), lambda h: (0, 0, h))
    sspec = pl.BlockSpec((None, tiles, 1, rows * tf), lambda h: (h, 0, 0, 0))
    pspec = pl.BlockSpec((2, rows, width, HEAD_DIM), lambda h: (0, 0, 0, h))
    ispec = pl.BlockSpec((2, 2, rows, width, HEAD_DIM), lambda h: (0, 0, 0, 0, h))
    pairs = tiles * rows * tf * krows * (tf + 2 * mf) * heads
    cost = pl.CostEstimate(
        flops=10 * pairs * HEAD_DIM,
        transcendentals=pairs,
        bytes_accessed=2 * (2 * q.size + 2 * k_ext.size + q.size) + 8 * krows * width * channels,
    )
    part = jax.ShapeDtypeStruct((2, rows, width, channels), jnp.float32)
    return pl.pallas_call(
        kernel,
        grid=(heads,),
        in_specs=[qspec, qspec, sspec, sspec, kspec, kspec],
        out_specs=[qspec, pspec, ispec, pspec],
        out_shape=[
            jax.ShapeDtypeStruct((rows, width, channels), jnp.bfloat16),
            part,
            jax.ShapeDtypeStruct((2, 2, rows, width, channels), jnp.float32),
            part,
        ],
        cost_estimate=cost,
    )(q, do, lse_t, delta_t, k_ext, v_ext)


def stats_tiles(stats, tiles, tf):
    rows, width, heads = stats.shape
    tiled = stats.reshape(rows, tiles, tf, heads)
    tiled = jnp.transpose(tiled, (3, 1, 0, 2))
    return tiled.reshape(heads, tiles, 1, rows * tf)


def on_device(queries, key_vecs, value_vecs, outputs_fwd, grad_out, log_norm):
    rows, width_cells, frames, channels = queries.shape
    heads = log_norm.shape[3]
    width = width_cells * frames
    tiles = width_cells // TILE
    tf = TILE * frames
    mf = MARGIN * frames

    q = queries.reshape(rows, width, channels)
    do = grad_out.reshape(rows, width, channels)
    row_delta = jnp.einsum(
        "rwhd,rwhd->rwh",
        grad_out.reshape(rows, width, heads, HEAD_DIM),
        outputs_fwd.reshape(rows, width, heads, HEAD_DIM),
        preferred_element_type=jnp.float32,
    )
    lse_t = stats_tiles(log_norm.reshape(rows, width, heads), tiles, tf)
    delta_t = stats_tiles(row_delta, tiles, tf)

    kv_own = (key_vecs.reshape(rows, width, channels), value_vecs.reshape(rows, width, channels))
    kv_partner = swap(kv_own, core_partner)
    kv_cross = swap(kv_own, chip_neighbour)
    kv_forward = swap(kv_cross, core_partner)

    def extended(member):
        joined = jnp.concatenate(
            [kv_own[member], kv_partner[member], kv_cross[member], kv_forward[member]], axis=0
        )
        return jnp.concatenate([joined[:, width - mf :], joined, joined[:, :mf]], axis=1)

    dq, own, intra, cross = window_pass(q, do, lse_t, delta_t, extended(0), extended(1), tiles, tf, mf)

    back = swap(intra, core_partner)
    own_total = own + back[0]
    cross_total = (cross + back[1]).astype(jnp.bfloat16)
    arrived = swap(cross_total, chip_neighbour)
    total = own_total + arrived.astype(jnp.float32)
    grad_keys = total[0].astype(jnp.bfloat16).reshape(rows, width_cells, frames, channels)
    grad_values = total[1].astype(jnp.bfloat16).reshape(rows, width_cells, frames, channels)
    grad_queries = dq.reshape(rows, width_cells, frames, channels)
    return (grad_queries, grad_keys, grad_values)


def solution(mesh):
    spec = P("sy", "groups", None, None)
    return jax.shard_map(
        on_device,
        mesh=mesh,
        in_specs=(spec,) * 6,
        out_specs=(spec,) * 3,
        check_vma=False,
    )
```

```python
import functools

import jax
import jax.numpy as jnp
from jax import lax
from jax.experimental import pallas as pl
from jax.experimental.pallas import tpu as pltpu
from jax.sharding import PartitionSpec as P

HEAD_DIM = 128
TILE = 8
MARGIN = 4


def swap(block, pairs_of):
    n = lax.axis_size("sy")
    route = []
    for i in range(n):
        route.append((i, pairs_of(i, n)))
    return lax.ppermute(block, "sy", route)


def core_partner(i, n):
    return i ^ 1


def chip_neighbour(i, n):
    return (i + 1) % n if i % 2 else (i - 1) % n


def window_kernel(
    q_ref, do_ref, lse_ref, delta_ref, k_ref, v_ref, dq_ref, own_ref, intra_ref, cross_ref, *, tiles, tf, mf
):
    scaling = HEAD_DIM ** (-0.5)
    rows = q_ref.shape[0]
    krows = k_ref.shape[0]
    width = own_ref.shape[2]
    span = tf + 2 * mf
    own_ref[...] = jnp.zeros_like(own_ref)
    intra_ref[...] = jnp.zeros_like(intra_ref)
    cross_ref[...] = jnp.zeros_like(cross_ref)
    targets = [own_ref, intra_ref.at[0], cross_ref, intra_ref.at[1]]
    blocks = krows // rows
    for b in range(tiles):
        kw = k_ref[:, b * tf : b * tf + span, :].reshape(krows * span, HEAD_DIM)
        vw = v_ref[:, b * tf : b * tf + span, :].reshape(krows * span, HEAD_DIM)
        qb = q_ref[:, b * tf : (b + 1) * tf, :].reshape(rows * tf, HEAD_DIM)
        dob = do_ref[:, b * tf : (b + 1) * tf, :].reshape(rows * tf, HEAD_DIM)
        nt = (((1,), (1,)), ((), ()))
        scores = lax.dot_general(kw, qb, nt, preferred_element_type=jnp.float32) * scaling
        attention = jnp.exp(scores - lse_ref[b])
        grad_attention = lax.dot_general(vw, dob, nt, preferred_element_type=jnp.float32)
        grad_scores = (attention * (grad_attention - delta_ref[b])).astype(jnp.bfloat16)
        grad_v = jnp.dot(attention.astype(jnp.bfloat16), dob, preferred_element_type=jnp.float32)
        grad_k = jnp.dot(grad_scores, qb, preferred_element_type=jnp.float32) * scaling
        grad_q = jnp.dot(grad_scores.T, kw, preferred_element_type=jnp.float32) * scaling
        dq_ref[:, b * tf : (b + 1) * tf, :] = grad_q.reshape(rows, tf, HEAD_DIM).astype(dq_ref.dtype)
        grad_k = grad_k.reshape(blocks, rows, span, HEAD_DIM)
        grad_v = grad_v.reshape(blocks, rows, span, HEAD_DIM)
        start = b * tf - mf
        pieces = []
        if start < 0:
            pieces.append((0, width + start, -start))
            pieces.append((-start, 0, span + start))
        elif start + span > width:
            pieces.append((0, start, width - start))
            pieces.append((width - start, 0, start + span - width))
        else:
            pieces.append((0, start, span))
        for block, target in enumerate(targets):
            for src, dst, size in pieces:
                target[0, :, dst : dst + size, :] += grad_k[block, :, src : src + size, :]
                target[1, :, dst : dst + size, :] += grad_v[block, :, src : src + size, :]


def window_pass(q, do, lse_t, delta_t, k_ext, v_ext, tiles, tf, mf, first):
    rows, width, _ = q.shape
    krows = k_ext.shape[0]
    ext = k_ext.shape[1]
    channels = k_ext.shape[2]
    heads = channels // HEAD_DIM
    kernel = functools.partial(window_kernel, tiles=tiles, tf=tf, mf=mf)
    qspec = pl.BlockSpec((rows, width, HEAD_DIM), lambda h: (0, 0, h + first))
    dqspec = pl.BlockSpec((rows, width, HEAD_DIM), lambda h: (0, 0, h))
    kspec = pl.BlockSpec((krows, ext, HEAD_DIM), lambda h: (0, 0, h))
    sspec = pl.BlockSpec((None, tiles, 1, rows * tf), lambda h: (h + first, 0, 0, 0))
    pspec = pl.BlockSpec((2, rows, width, HEAD_DIM), lambda h: (0, 0, 0, h))
    ispec = pl.BlockSpec((2, 2, rows, width, HEAD_DIM), lambda h: (0, 0, 0, 0, h))
    pairs = tiles * rows * tf * krows * (tf + 2 * mf) * heads
    cost = pl.CostEstimate(
        flops=10 * pairs * HEAD_DIM,
        transcendentals=pairs,
        bytes_accessed=2 * (3 * rows * width * channels + 2 * k_ext.size) + 8 * krows * width * channels,
    )
    part = jax.ShapeDtypeStruct((2, rows, width, channels), jnp.float32)
    return pl.pallas_call(
        kernel,
        grid=(heads,),
        in_specs=[qspec, qspec, sspec, sspec, kspec, kspec],
        out_specs=[dqspec, pspec, ispec, pspec],
        out_shape=[
            jax.ShapeDtypeStruct((rows, width, channels), jnp.bfloat16),
            part,
            jax.ShapeDtypeStruct((2, 2, rows, width, channels), jnp.float32),
            part,
        ],
        cost_estimate=cost,
    )(q, do, lse_t, delta_t, k_ext, v_ext)


def stats_tiles(stats, tiles, tf):
    rows, width, heads = stats.shape
    tiled = stats.reshape(rows, tiles, tf, heads)
    tiled = jnp.transpose(tiled, (3, 1, 0, 2))
    return tiled.reshape(heads, tiles, 1, rows * tf)


def on_device(queries, key_vecs, value_vecs, outputs_fwd, grad_out, log_norm):
    rows, width_cells, frames, channels = queries.shape
    heads = log_norm.shape[3]
    width = width_cells * frames
    tiles = width_cells // TILE
    tf = TILE * frames
    mf = MARGIN * frames

    q = queries.reshape(rows, width, channels)
    do = grad_out.reshape(rows, width, channels)
    row_delta = jnp.einsum(
        "rwhd,rwhd->rwh",
        grad_out.reshape(rows, width, heads, HEAD_DIM),
        outputs_fwd.reshape(rows, width, heads, HEAD_DIM),
        preferred_element_type=jnp.float32,
    )
    lse_t = stats_tiles(log_norm.reshape(rows, width, heads), tiles, tf)
    delta_t = stats_tiles(row_delta, tiles, tf)

    chunks = 2 if heads % 2 == 0 else 1
    size = channels // chunks
    dq_parts = []
    total_parts = []
    for chunk in range(chunks):
        columns = slice(chunk * size, (chunk + 1) * size)
        kv_own = (
            key_vecs[..., columns].reshape(rows, width, size),
            value_vecs[..., columns].reshape(rows, width, size),
        )
        kv_partner = swap(kv_own, core_partner)
        kv_cross = swap(kv_own, chip_neighbour)
        kv_forward = swap(kv_cross, core_partner)

        def extended(member):
            joined = jnp.concatenate(
                [kv_own[member], kv_partner[member], kv_cross[member], kv_forward[member]], axis=0
            )
            return jnp.concatenate([joined[:, width - mf :], joined, joined[:, :mf]], axis=1)

        first = chunk * (heads // chunks)
        dq, own, intra, cross = window_pass(
            q, do, lse_t, delta_t, extended(0), extended(1), tiles, tf, mf, first
        )
        back = swap(intra, core_partner)
        own_total = own + back[0]
        cross_total = (cross + back[1]).astype(jnp.bfloat16)
        arrived = swap(cross_total, chip_neighbour)
        dq_parts.append(dq)
        total_parts.append(own_total + arrived.astype(jnp.float32))
    total = jnp.concatenate(total_parts, axis=-1)
    dq = jnp.concatenate(dq_parts, axis=-1)
    grad_keys = total[0].astype(jnp.bfloat16).reshape(rows, width_cells, frames, channels)
    grad_values = total[1].astype(jnp.bfloat16).reshape(rows, width_cells, frames, channels)
    grad_queries = dq.reshape(rows, width_cells, frames, channels)
    return (grad_queries, grad_keys, grad_values)


def solution(mesh):
    spec = P("sy", "groups", None, None)
    return jax.shard_map(
        on_device,
        mesh=mesh,
        in_specs=(spec,) * 6,
        out_specs=(spec,) * 3,
        check_vma=False,
    )
```

```python
import functools

import jax
import jax.numpy as jnp
from jax import lax
from jax.experimental import pallas as pl
from jax.experimental.pallas import tpu as pltpu
from jax.sharding import PartitionSpec as P

HEAD_DIM = 128
TILE = 8
MARGIN = 4


def swap(block, pairs_of):
    n = lax.axis_size("sy")
    route = []
    for i in range(n):
        route.append((i, pairs_of(i, n)))
    return lax.ppermute(block, "sy", route)


def core_partner(i, n):
    return i ^ 1


def chip_neighbour(i, n):
    return (i + 1) % n if i % 2 else (i - 1) % n


def window_kernel(*refs, tiles, tf, mf, accumulate):
    if accumulate:
        q_ref, do_ref, lse_ref, delta_ref, k_ref, v_ref, dqin_ref, dq_ref, first_ref, second_ref = refs
    else:
        q_ref, do_ref, lse_ref, delta_ref, k_ref, v_ref, dq_ref, first_ref, second_ref = refs
        dqin_ref = None
    scaling = HEAD_DIM ** (-0.5)
    rows = q_ref.shape[0]
    krows = k_ref.shape[0]
    width = first_ref.shape[2]
    span = tf + 2 * mf
    first_ref[...] = jnp.zeros_like(first_ref)
    second_ref[...] = jnp.zeros_like(second_ref)
    targets = [first_ref, second_ref]
    blocks = krows // rows
    for b in range(tiles):
        kw = k_ref[:, b * tf : b * tf + span, :].reshape(krows * span, HEAD_DIM)
        vw = v_ref[:, b * tf : b * tf + span, :].reshape(krows * span, HEAD_DIM)
        qb = q_ref[:, b * tf : (b + 1) * tf, :].reshape(rows * tf, HEAD_DIM)
        dob = do_ref[:, b * tf : (b + 1) * tf, :].reshape(rows * tf, HEAD_DIM)
        nt = (((1,), (1,)), ((), ()))
        scores = lax.dot_general(kw, qb, nt, preferred_element_type=jnp.float32) * scaling
        attention = jnp.exp(scores - lse_ref[b])
        grad_attention = lax.dot_general(vw, dob, nt, preferred_element_type=jnp.float32)
        grad_scores = (attention * (grad_attention - delta_ref[b])).astype(jnp.bfloat16)
        grad_v = jnp.dot(attention.astype(jnp.bfloat16), dob, preferred_element_type=jnp.float32)
        grad_k = jnp.dot(grad_scores, qb, preferred_element_type=jnp.float32) * scaling
        grad_q = jnp.dot(grad_scores.T, kw, preferred_element_type=jnp.float32) * scaling
        grad_q = grad_q.reshape(rows, tf, HEAD_DIM)
        if dqin_ref is not None:
            grad_q = grad_q + dqin_ref[:, b * tf : (b + 1) * tf, :]
        dq_ref[:, b * tf : (b + 1) * tf, :] = grad_q.astype(dq_ref.dtype)
        grad_k = grad_k.reshape(blocks, rows, span, HEAD_DIM)
        grad_v = grad_v.reshape(blocks, rows, span, HEAD_DIM)
        start = b * tf - mf
        pieces = []
        if start < 0:
            pieces.append((0, width + start, -start))
            pieces.append((-start, 0, span + start))
        elif start + span > width:
            pieces.append((0, start, width - start))
            pieces.append((width - start, 0, start + span - width))
        else:
            pieces.append((0, start, span))
        for block, target in enumerate(targets):
            for src, dst, size in pieces:
                target[0, :, dst : dst + size, :] += grad_k[block, :, src : src + size, :]
                target[1, :, dst : dst + size, :] += grad_v[block, :, src : src + size, :]


def window_pass(q, do, lse_t, delta_t, k_ext, v_ext, dq_in, tiles, tf, mf):
    rows, width, channels = q.shape
    krows = k_ext.shape[0]
    ext = k_ext.shape[1]
    heads = channels // HEAD_DIM
    accumulate = dq_in is not None
    kernel = functools.partial(window_kernel, tiles=tiles, tf=tf, mf=mf, accumulate=accumulate)
    qspec = pl.BlockSpec((rows, width, HEAD_DIM), lambda h: (0, 0, h))
    kspec = pl.BlockSpec((krows, ext, HEAD_DIM), lambda h: (0, 0, h))
    sspec = pl.BlockSpec((None, tiles, 1, rows * tf), lambda h: (h, 0, 0, 0))
    pspec = pl.BlockSpec((2, rows, width, HEAD_DIM), lambda h: (0, 0, 0, h))
    pairs = tiles * rows * tf * krows * (tf + 2 * mf) * heads
    cost = pl.CostEstimate(
        flops=10 * pairs * HEAD_DIM,
        transcendentals=pairs,
        bytes_accessed=2 * (2 * q.size + 2 * k_ext.size + q.size) + 12 * krows * width * channels,
    )
    part = jax.ShapeDtypeStruct((2, rows, width, channels), jnp.float32)
    dq_type = jnp.bfloat16 if accumulate else jnp.float32
    operands = [q, do, lse_t, delta_t, k_ext, v_ext]
    in_specs = [qspec, qspec, sspec, sspec, kspec, kspec]
    if accumulate:
        operands.append(dq_in)
        in_specs.append(qspec)
    return pl.pallas_call(
        kernel,
        grid=(heads,),
        in_specs=in_specs,
        out_specs=[qspec, pspec, pspec],
        out_shape=[jax.ShapeDtypeStruct((rows, width, channels), dq_type), part, part],
        cost_estimate=cost,
    )(*operands)


def stats_tiles(stats, tiles, tf):
    rows, width, heads = stats.shape
    tiled = stats.reshape(rows, tiles, tf, heads)
    tiled = jnp.transpose(tiled, (3, 1, 0, 2))
    return tiled.reshape(heads, tiles, 1, rows * tf)


def on_device(queries, key_vecs, value_vecs, outputs_fwd, grad_out, log_norm):
    rows, width_cells, frames, channels = queries.shape
    heads = log_norm.shape[3]
    width = width_cells * frames
    tiles = width_cells // TILE
    tf = TILE * frames
    mf = MARGIN * frames

    q = queries.reshape(rows, width, channels)
    do = grad_out.reshape(rows, width, channels)
    row_delta = jnp.einsum(
        "rwhd,rwhd->rwh",
        grad_out.reshape(rows, width, heads, HEAD_DIM),
        outputs_fwd.reshape(rows, width, heads, HEAD_DIM),
        preferred_element_type=jnp.float32,
    )
    lse_t = stats_tiles(log_norm.reshape(rows, width, heads), tiles, tf)
    delta_t = stats_tiles(row_delta, tiles, tf)

    kv_own = (key_vecs.reshape(rows, width, channels), value_vecs.reshape(rows, width, channels))
    kv_partner = swap(kv_own, core_partner)
    kv_cross = swap(kv_own, chip_neighbour)

    def extended(upper, lower, member):
        joined = jnp.concatenate([upper[member], lower[member]], axis=0)
        return jnp.concatenate([joined[:, width - mf :], joined, joined[:, :mf]], axis=1)

    dq_local, part_own, part_partner = window_pass(
        q, do, lse_t, delta_t,
        extended(kv_own, kv_partner, 0), extended(kv_own, kv_partner, 1),
        None, tiles, tf, mf,
    )
    kv_cross, dq_local = lax.optimization_barrier((kv_cross, dq_local))
    kv_forward = swap(kv_cross, core_partner)
    back_partner = swap(part_partner, core_partner)
    dq, part_cross, part_forward = window_pass(
        q, do, lse_t, delta_t,
        extended(kv_cross, kv_forward, 0), extended(kv_cross, kv_forward, 1),
        dq_local, tiles, tf, mf,
    )
    back_forward = swap(part_forward, core_partner)
    own_total = part_own + back_partner
    cross_total = (part_cross + back_forward).astype(jnp.bfloat16)
    arrived = swap(cross_total, chip_neighbour)
    total = own_total + arrived.astype(jnp.float32)
    grad_keys = total[0].astype(jnp.bfloat16).reshape(rows, width_cells, frames, channels)
    grad_values = total[1].astype(jnp.bfloat16).reshape(rows, width_cells, frames, channels)
    grad_queries = dq.reshape(rows, width_cells, frames, channels)
    return (grad_queries, grad_keys, grad_values)


def solution(mesh):
    spec = P("sy", "groups", None, None)
    return jax.shard_map(
        on_device,
        mesh=mesh,
        in_specs=(spec,) * 6,
        out_specs=(spec,) * 3,
        check_vma=False,
    )
```

```python
import functools

import jax
import jax.numpy as jnp
from jax import lax
from jax.experimental import pallas as pl
from jax.experimental.pallas import tpu as pltpu
from jax.sharding import PartitionSpec as P

HEAD_DIM = 128
TILE = 8
MARGIN = 4


def swap(block, pairs_of):
    n = lax.axis_size("sy")
    route = []
    for i in range(n):
        route.append((i, pairs_of(i, n)))
    return lax.ppermute(block, "sy", route)


def core_partner(i, n):
    return i ^ 1


def chip_neighbour(i, n):
    return (i + 1) % n if i % 2 else (i - 1) % n


def window_pieces(start, span, width):
    if start + span <= width:
        return [(0, start, span)]
    return [(0, start, width - start), (width - start, 0, start + span - width)]


def window_kernel(*refs, tiles, tf, mf, accumulate):
    if accumulate:
        q_ref, do_ref, lse_ref, delta_ref, ka_ref, kb_ref, va_ref, vb_ref, dqin_ref = refs[:9]
    else:
        q_ref, do_ref, lse_ref, delta_ref, ka_ref, kb_ref, va_ref, vb_ref = refs[:8]
        dqin_ref = None
    dq_ref, first_ref, second_ref = refs[-3:]
    scaling = HEAD_DIM ** (-0.5)
    rows = q_ref.shape[0]
    width = first_ref.shape[2]
    span = tf + 2 * mf
    first_ref[...] = jnp.zeros_like(first_ref)
    second_ref[...] = jnp.zeros_like(second_ref)
    targets = [first_ref, second_ref]

    def window(refs_pair, pieces):
        parts = []
        for ref in refs_pair:
            slabs = [ref[:, dst : dst + size, :] for _, dst, size in pieces]
            parts.append(slabs[0] if len(slabs) == 1 else jnp.concatenate(slabs, axis=1))
        return jnp.concatenate(parts, axis=0).reshape(len(refs_pair) * rows * span, HEAD_DIM)

    for b in range(tiles):
        pieces = window_pieces(b * tf, span, width)
        kw = window((ka_ref, kb_ref), pieces)
        vw = window((va_ref, vb_ref), pieces)
        qb = q_ref[:, b * tf : (b + 1) * tf, :].reshape(rows * tf, HEAD_DIM)
        dob = do_ref[:, b * tf : (b + 1) * tf, :].reshape(rows * tf, HEAD_DIM)
        nt = (((1,), (1,)), ((), ()))
        scores = lax.dot_general(kw, qb, nt, preferred_element_type=jnp.float32) * scaling
        attention = jnp.exp(scores - lse_ref[b])
        grad_attention = lax.dot_general(vw, dob, nt, preferred_element_type=jnp.float32)
        grad_scores = (attention * (grad_attention - delta_ref[b])).astype(jnp.bfloat16)
        grad_v = jnp.dot(attention.astype(jnp.bfloat16), dob, preferred_element_type=jnp.float32)
        grad_k = jnp.dot(grad_scores, qb, preferred_element_type=jnp.float32) * scaling
        grad_q = jnp.dot(grad_scores.T, kw, preferred_element_type=jnp.float32) * scaling
        grad_q = grad_q.reshape(rows, tf, HEAD_DIM)
        if dqin_ref is not None:
            grad_q = grad_q + dqin_ref[:, b * tf : (b + 1) * tf, :]
        dq_ref[:, b * tf : (b + 1) * tf, :] = grad_q.astype(dq_ref.dtype)
        grad_k = grad_k.reshape(2, rows, span, HEAD_DIM)
        grad_v = grad_v.reshape(2, rows, span, HEAD_DIM)
        for block, target in enumerate(targets):
            for src, dst, size in pieces:
                target[0, :, dst : dst + size, :] += grad_k[block, :, src : src + size, :]
                target[1, :, dst : dst + size, :] += grad_v[block, :, src : src + size, :]


def window_pass(q, do, lse_t, delta_t, kv_a, kv_b, dq_in, tiles, tf, mf):
    rows, width, channels = q.shape
    heads = channels // HEAD_DIM
    accumulate = dq_in is not None
    kernel = functools.partial(window_kernel, tiles=tiles, tf=tf, mf=mf, accumulate=accumulate)
    qspec = pl.BlockSpec((rows, width, HEAD_DIM), lambda h: (0, 0, h))
    sspec = pl.BlockSpec((None, tiles, 1, rows * tf), lambda h: (h, 0, 0, 0))
    pspec = pl.BlockSpec((2, rows, width, HEAD_DIM), lambda h: (0, 0, 0, h))
    pairs = tiles * rows * tf * 2 * rows * (tf + 2 * mf) * heads
    cost = pl.CostEstimate(
        flops=10 * pairs * HEAD_DIM,
        transcendentals=pairs,
        bytes_accessed=2 * 7 * q.size + 24 * q.size,
    )
    part = jax.ShapeDtypeStruct((2, rows, width, channels), jnp.float32)
    dq_type = jnp.bfloat16 if accumulate else jnp.float32
    operands = [q, do, lse_t, delta_t, kv_a[0], kv_b[0], kv_a[1], kv_b[1]]
    in_specs = [qspec, qspec, sspec, sspec, qspec, qspec, qspec, qspec]
    if accumulate:
        operands.append(dq_in)
        in_specs.append(qspec)
    return pl.pallas_call(
        kernel,
        grid=(heads,),
        in_specs=in_specs,
        out_specs=[qspec, pspec, pspec],
        out_shape=[jax.ShapeDtypeStruct((rows, width, channels), dq_type), part, part],
        cost_estimate=cost,
    )(*operands)


def stats_tiles(stats, tiles, tf):
    rows, width, heads = stats.shape
    tiled = stats.reshape(rows, tiles, tf, heads)
    tiled = jnp.transpose(tiled, (3, 1, 0, 2))
    return tiled.reshape(heads, tiles, 1, rows * tf)


def on_device(queries, key_vecs, value_vecs, outputs_fwd, grad_out, log_norm):
    rows, width_cells, frames, channels = queries.shape
    heads = log_norm.shape[3]
    width = width_cells * frames
    tiles = width_cells // TILE
    tf = TILE * frames
    mf = MARGIN * frames

    q = queries.reshape(rows, width, channels)
    do = grad_out.reshape(rows, width, channels)
    row_delta = jnp.einsum(
        "rwhd,rwhd->rwh",
        grad_out.reshape(rows, width, heads, HEAD_DIM),
        outputs_fwd.reshape(rows, width, heads, HEAD_DIM),
        preferred_element_type=jnp.float32,
    )
    lse_t = stats_tiles(log_norm.reshape(rows, width, heads), tiles, tf)
    delta_t = stats_tiles(row_delta, tiles, tf)

    kv_own = (
        jnp.roll(key_vecs.reshape(rows, width, channels), mf, axis=1),
        jnp.roll(value_vecs.reshape(rows, width, channels), mf, axis=1),
    )
    kv_partner = swap(kv_own, core_partner)
    kv_cross = swap(kv_own, chip_neighbour)

    dq_local, part_own, part_partner = window_pass(
        q, do, lse_t, delta_t, kv_own, kv_partner, None, tiles, tf, mf
    )
    kv_cross, dq_local = lax.optimization_barrier((kv_cross, dq_local))
    kv_forward = swap(kv_cross, core_partner)
    back_partner = swap(part_partner, core_partner)
    dq, part_cross, part_forward = window_pass(
        q, do, lse_t, delta_t, kv_cross, kv_forward, dq_local, tiles, tf, mf
    )
    back_forward = swap(part_forward, core_partner)
    own_total = part_own + back_partner
    cross_total = (part_cross + back_forward).astype(jnp.bfloat16)
    arrived = swap(cross_total, chip_neighbour)
    total = jnp.roll(own_total + arrived.astype(jnp.float32), -mf, axis=2)
    grad_keys = total[0].astype(jnp.bfloat16).reshape(rows, width_cells, frames, channels)
    grad_values = total[1].astype(jnp.bfloat16).reshape(rows, width_cells, frames, channels)
    grad_queries = dq.reshape(rows, width_cells, frames, channels)
    return (grad_queries, grad_keys, grad_values)


def solution(mesh):
    spec = P("sy", "groups", None, None)
    return jax.shard_map(
        on_device,
        mesh=mesh,
        in_specs=(spec,) * 6,
        out_specs=(spec,) * 3,
        check_vma=False,
    )
```

```python
import functools

import jax
import jax.numpy as jnp
from jax import lax
from jax.experimental import pallas as pl
from jax.experimental.pallas import tpu as pltpu
from jax.sharding import PartitionSpec as P

HEAD_DIM = 128
TILE = 8
MARGIN = 4


def swap(block, pairs_of):
    n = lax.axis_size("sy")
    route = []
    for i in range(n):
        route.append((i, pairs_of(i, n)))
    return lax.ppermute(block, "sy", route)


def core_partner(i, n):
    return i ^ 1


def chip_neighbour(i, n):
    return (i + 1) % n if i % 2 else (i - 1) % n


def window_pieces(start, span, width):
    if start + span <= width:
        return [(0, start, span)]
    return [(0, start, width - start), (width - start, 0, start + span - width)]


def window_kernel(*refs, tiles, tf, mf, accumulate):
    if accumulate:
        q_ref, do_ref, lse_ref, delta_ref, ka_ref, kb_ref, va_ref, vb_ref, dqin_ref = refs[:9]
    else:
        q_ref, do_ref, lse_ref, delta_ref, ka_ref, kb_ref, va_ref, vb_ref = refs[:8]
        dqin_ref = None
    dq_ref, first_ref, second_ref = refs[-3:]
    scaling = HEAD_DIM ** (-0.5)
    rows = q_ref.shape[0]
    width = first_ref.shape[2]
    span = tf + 2 * mf
    first_ref[...] = jnp.zeros_like(first_ref)
    second_ref[...] = jnp.zeros_like(second_ref)
    targets = [first_ref, second_ref]

    def window(refs_pair, pieces):
        parts = []
        for ref in refs_pair:
            slabs = [ref[:, dst : dst + size, :] for _, dst, size in pieces]
            parts.append(slabs[0] if len(slabs) == 1 else jnp.concatenate(slabs, axis=1))
        return jnp.concatenate(parts, axis=0).reshape(len(refs_pair) * rows * span, HEAD_DIM)

    for b in range(tiles):
        pieces = window_pieces(b * tf, span, width)
        kw = window((ka_ref, kb_ref), pieces)
        vw = window((va_ref, vb_ref), pieces)
        qb = q_ref[:, b * tf : (b + 1) * tf, :].reshape(rows * tf, HEAD_DIM)
        dob = do_ref[:, b * tf : (b + 1) * tf, :].reshape(rows * tf, HEAD_DIM)
        nt = (((1,), (1,)), ((), ()))
        scores = lax.dot_general(kw, qb, nt, preferred_element_type=jnp.float32) * scaling
        attention = jnp.exp(scores - lse_ref[b])
        grad_attention = lax.dot_general(vw, dob, nt, preferred_element_type=jnp.float32)
        grad_scores = (attention * (grad_attention - delta_ref[b])).astype(jnp.bfloat16)
        grad_v = jnp.dot(attention.astype(jnp.bfloat16), dob, preferred_element_type=jnp.float32)
        grad_k = jnp.dot(grad_scores, qb, preferred_element_type=jnp.float32) * scaling
        grad_q = jnp.dot(grad_scores.T, kw, preferred_element_type=jnp.float32) * scaling
        grad_q = grad_q.reshape(rows, tf, HEAD_DIM)
        if dqin_ref is not None:
            grad_q = grad_q + dqin_ref[:, b * tf : (b + 1) * tf, :]
        dq_ref[:, b * tf : (b + 1) * tf, :] = grad_q.astype(dq_ref.dtype)
        grad_k = grad_k.reshape(2, rows, span, HEAD_DIM)
        grad_v = grad_v.reshape(2, rows, span, HEAD_DIM)
        for block, target in enumerate(targets):
            for src, dst, size in pieces:
                target[0, :, dst : dst + size, :] += grad_k[block, :, src : src + size, :]
                target[1, :, dst : dst + size, :] += grad_v[block, :, src : src + size, :]


def window_pass(q, do, lse_t, delta_t, kv_a, kv_b, dq_in, tiles, tf, mf, first=0, heads=None):
    rows, width, all_channels = q.shape
    if heads is None:
        heads = all_channels // HEAD_DIM
    channels = heads * HEAD_DIM
    accumulate = dq_in is not None
    kernel = functools.partial(window_kernel, tiles=tiles, tf=tf, mf=mf, accumulate=accumulate)
    qspec = pl.BlockSpec((rows, width, HEAD_DIM), lambda h: (0, 0, h + first))
    dqspec = pl.BlockSpec((rows, width, HEAD_DIM), lambda h: (0, 0, h))
    sspec = pl.BlockSpec((None, tiles, 1, rows * tf), lambda h: (h + first, 0, 0, 0))
    pspec = pl.BlockSpec((2, rows, width, HEAD_DIM), lambda h: (0, 0, 0, h))
    pairs = tiles * rows * tf * 2 * rows * (tf + 2 * mf) * heads
    cost = pl.CostEstimate(
        flops=10 * pairs * HEAD_DIM,
        transcendentals=pairs,
        bytes_accessed=38 * rows * width * channels,
    )
    part = jax.ShapeDtypeStruct((2, rows, width, channels), jnp.float32)
    dq_type = jnp.bfloat16 if accumulate else jnp.float32
    operands = [q, do, lse_t, delta_t, kv_a[0], kv_b[0], kv_a[1], kv_b[1]]
    in_specs = [qspec, qspec, sspec, sspec, qspec, qspec, qspec, qspec]
    if accumulate:
        operands.append(dq_in)
        in_specs.append(qspec)
    return pl.pallas_call(
        kernel,
        grid=(heads,),
        in_specs=in_specs,
        out_specs=[dqspec, pspec, pspec],
        out_shape=[jax.ShapeDtypeStruct((rows, width, channels), dq_type), part, part],
        cost_estimate=cost,
    )(*operands)


def stats_tiles(stats, tiles, tf):
    rows, width, heads = stats.shape
    tiled = stats.reshape(rows, tiles, tf, heads)
    tiled = jnp.transpose(tiled, (3, 1, 0, 2))
    return tiled.reshape(heads, tiles, 1, rows * tf)


def on_device(queries, key_vecs, value_vecs, outputs_fwd, grad_out, log_norm):
    rows, width_cells, frames, channels = queries.shape
    heads = log_norm.shape[3]
    width = width_cells * frames
    tiles = width_cells // TILE
    tf = TILE * frames
    mf = MARGIN * frames

    q = queries.reshape(rows, width, channels)
    do = grad_out.reshape(rows, width, channels)
    row_delta = jnp.einsum(
        "rwhd,rwhd->rwh",
        grad_out.reshape(rows, width, heads, HEAD_DIM),
        outputs_fwd.reshape(rows, width, heads, HEAD_DIM),
        preferred_element_type=jnp.float32,
    )
    lse_t = stats_tiles(log_norm.reshape(rows, width, heads), tiles, tf)
    delta_t = stats_tiles(row_delta, tiles, tf)

    kv_own = (
        jnp.roll(key_vecs.reshape(rows, width, channels), mf, axis=1),
        jnp.roll(value_vecs.reshape(rows, width, channels), mf, axis=1),
    )
    kv_partner = swap(kv_own, core_partner)
    kv_cross = swap(kv_own, chip_neighbour)

    dq_local, part_own, part_partner = window_pass(
        q, do, lse_t, delta_t, kv_own, kv_partner, None, tiles, tf, mf
    )
    kv_cross, dq_local = lax.optimization_barrier((kv_cross, dq_local))
    kv_forward = swap(kv_cross, core_partner)
    back_partner = swap(part_partner, core_partner)
    own_total = part_own + back_partner
    halves = 2 if heads % 2 == 0 else 1
    count = heads // halves
    dq_parts = []
    arrived_parts = []
    for half in range(halves):
        dq_half, part_cross, part_forward = window_pass(
            q, do, lse_t, delta_t, kv_cross, kv_forward, dq_local, tiles, tf, mf,
            first=half * count, heads=count,
        )
        back_forward = swap(part_forward, core_partner)
        cross_total = (part_cross + back_forward).astype(jnp.bfloat16)
        arrived_parts.append(swap(cross_total, chip_neighbour).astype(jnp.float32))
        dq_parts.append(dq_half)
    dq = jnp.concatenate(dq_parts, axis=-1)
    total = jnp.roll(own_total + jnp.concatenate(arrived_parts, axis=-1), -mf, axis=2)
    grad_keys = total[0].astype(jnp.bfloat16).reshape(rows, width_cells, frames, channels)
    grad_values = total[1].astype(jnp.bfloat16).reshape(rows, width_cells, frames, channels)
    grad_queries = dq.reshape(rows, width_cells, frames, channels)
    return (grad_queries, grad_keys, grad_values)


def solution(mesh):
    spec = P("sy", "groups", None, None)
    return jax.shard_map(
        on_device,
        mesh=mesh,
        in_specs=(spec,) * 6,
        out_specs=(spec,) * 3,
        check_vma=False,
    )
```

```python
import functools

import jax
import jax.numpy as jnp
from jax import lax
from jax.experimental import pallas as pl
from jax.experimental.pallas import tpu as pltpu
from jax.sharding import PartitionSpec as P

HEAD_DIM = 128
TILE = 8
MARGIN = 4


def swap(block, pairs_of):
    n = lax.axis_size("sy")
    route = []
    for i in range(n):
        route.append((i, pairs_of(i, n)))
    return lax.ppermute(block, "sy", route)


def core_partner(i, n):
    return i ^ 1


def chip_neighbour(i, n):
    return (i + 1) % n if i % 2 else (i - 1) % n


def window_pieces(start, span, width):
    if start + span <= width:
        return [(0, start, span)]
    return [(0, start, width - start), (width - start, 0, start + span - width)]


def window_kernel(*refs, tiles, tf, mf, accumulate):
    if accumulate:
        q_ref, do_ref, lse_ref, delta_ref, ka_ref, kb_ref, va_ref, vb_ref, dqin_ref = refs[:9]
    else:
        q_ref, do_ref, lse_ref, delta_ref, ka_ref, kb_ref, va_ref, vb_ref = refs[:8]
        dqin_ref = None
    dq_ref, first_ref, second_ref = refs[-3:]
    scaling = HEAD_DIM ** (-0.5)
    rows = q_ref.shape[0]
    width = first_ref.shape[2]
    span = tf + 2 * mf
    first_ref[...] = jnp.zeros_like(first_ref)
    second_ref[...] = jnp.zeros_like(second_ref)
    targets = [first_ref, second_ref]

    def window(refs_pair, pieces):
        parts = []
        for ref in refs_pair:
            slabs = [ref[:, dst : dst + size, :] for _, dst, size in pieces]
            parts.append(slabs[0] if len(slabs) == 1 else jnp.concatenate(slabs, axis=1))
        return jnp.concatenate(parts, axis=0).reshape(len(refs_pair) * rows * span, HEAD_DIM)

    for b in range(tiles):
        pieces = window_pieces(b * tf, span, width)
        kw = window((ka_ref, kb_ref), pieces)
        vw = window((va_ref, vb_ref), pieces)
        qb = q_ref[:, b * tf : (b + 1) * tf, :].reshape(rows * tf, HEAD_DIM)
        dob = do_ref[:, b * tf : (b + 1) * tf, :].reshape(rows * tf, HEAD_DIM)
        nt = (((1,), (1,)), ((), ()))
        tn = (((0,), (0,)), ((), ()))
        scores = lax.dot_general(qb, kw, nt, preferred_element_type=jnp.float32) * scaling
        attention = jnp.exp(scores - lse_ref[b])
        grad_attention = lax.dot_general(dob, vw, nt, preferred_element_type=jnp.float32)
        grad_scores = (attention * (grad_attention - delta_ref[b])).astype(jnp.bfloat16)
        grad_v = lax.dot_general(
            attention.astype(jnp.bfloat16), dob, tn, preferred_element_type=jnp.float32
        )
        grad_k = lax.dot_general(grad_scores, qb, tn, preferred_element_type=jnp.float32) * scaling
        grad_q = jnp.dot(grad_scores, kw, preferred_element_type=jnp.float32) * scaling
        grad_q = grad_q.reshape(rows, tf, HEAD_DIM)
        if dqin_ref is not None:
            grad_q = grad_q + dqin_ref[:, b * tf : (b + 1) * tf, :]
        dq_ref[:, b * tf : (b + 1) * tf, :] = grad_q.astype(dq_ref.dtype)
        grad_k = grad_k.reshape(2, rows, span, HEAD_DIM)
        grad_v = grad_v.reshape(2, rows, span, HEAD_DIM)
        for block, target in enumerate(targets):
            for src, dst, size in pieces:
                target[0, :, dst : dst + size, :] += grad_k[block, :, src : src + size, :]
                target[1, :, dst : dst + size, :] += grad_v[block, :, src : src + size, :]


def window_pass(q, do, lse_t, delta_t, kv_a, kv_b, dq_in, tiles, tf, mf, first=0, heads=None):
    rows, width, all_channels = q.shape
    if heads is None:
        heads = all_channels // HEAD_DIM
    channels = heads * HEAD_DIM
    accumulate = dq_in is not None
    kernel = functools.partial(window_kernel, tiles=tiles, tf=tf, mf=mf, accumulate=accumulate)
    qspec = pl.BlockSpec((rows, width, HEAD_DIM), lambda h: (0, 0, h + first))
    dqspec = pl.BlockSpec((rows, width, HEAD_DIM), lambda h: (0, 0, h))
    sspec = pl.BlockSpec((None, tiles, rows * tf, 1), lambda h: (h + first, 0, 0, 0))
    pspec = pl.BlockSpec((2, rows, width, HEAD_DIM), lambda h: (0, 0, 0, h))
    pairs = tiles * rows * tf * 2 * rows * (tf + 2 * mf) * heads
    cost = pl.CostEstimate(
        flops=10 * pairs * HEAD_DIM,
        transcendentals=pairs,
        bytes_accessed=38 * rows * width * channels,
    )
    part = jax.ShapeDtypeStruct((2, rows, width, channels), jnp.float32)
    dq_type = jnp.bfloat16 if accumulate else jnp.float32
    operands = [q, do, lse_t, delta_t, kv_a[0], kv_b[0], kv_a[1], kv_b[1]]
    in_specs = [qspec, qspec, sspec, sspec, qspec, qspec, qspec, qspec]
    if accumulate:
        operands.append(dq_in)
        in_specs.append(qspec)
    return pl.pallas_call(
        kernel,
        grid=(heads,),
        in_specs=in_specs,
        out_specs=[dqspec, pspec, pspec],
        out_shape=[jax.ShapeDtypeStruct((rows, width, channels), dq_type), part, part],
        cost_estimate=cost,
    )(*operands)


def stats_tiles(stats, tiles, tf):
    rows, width, heads = stats.shape
    tiled = stats.reshape(rows, tiles, tf, heads)
    tiled = jnp.transpose(tiled, (3, 1, 0, 2))
    return tiled.reshape(heads, tiles, rows * tf, 1)


def on_device(queries, key_vecs, value_vecs, outputs_fwd, grad_out, log_norm):
    rows, width_cells, frames, channels = queries.shape
    heads = log_norm.shape[3]
    width = width_cells * frames
    tiles = width_cells // TILE
    tf = TILE * frames
    mf = MARGIN * frames

    q = queries.reshape(rows, width, channels)
    do = grad_out.reshape(rows, width, channels)
    row_delta = jnp.einsum(
        "rwhd,rwhd->rwh",
        grad_out.reshape(rows, width, heads, HEAD_DIM),
        outputs_fwd.reshape(rows, width, heads, HEAD_DIM),
        preferred_element_type=jnp.float32,
    )
    lse_t = stats_tiles(log_norm.reshape(rows, width, heads), tiles, tf)
    delta_t = stats_tiles(row_delta, tiles, tf)

    kv_own = (
        jnp.roll(key_vecs.reshape(rows, width, channels), mf, axis=1),
        jnp.roll(value_vecs.reshape(rows, width, channels), mf, axis=1),
    )
    kv_partner = swap(kv_own, core_partner)
    kv_cross = swap(kv_own, chip_neighbour)

    dq_local, part_own, part_partner = window_pass(
        q, do, lse_t, delta_t, kv_own, kv_partner, None, tiles, tf, mf
    )
    kv_cross, dq_local = lax.optimization_barrier((kv_cross, dq_local))
    kv_forward = swap(kv_cross, core_partner)
    back_partner = swap(part_partner, core_partner)
    own_total = part_own + back_partner
    halves = 2 if heads % 2 == 0 else 1
    count = heads // halves
    dq_parts = []
    arrived_parts = []
    for half in range(halves):
        dq_half, part_cross, part_forward = window_pass(
            q, do, lse_t, delta_t, kv_cross, kv_forward, dq_local, tiles, tf, mf,
            first=half * count, heads=count,
        )
        back_forward = swap(part_forward, core_partner)
        cross_total = (part_cross + back_forward).astype(jnp.bfloat16)
        arrived_parts.append(swap(cross_total, chip_neighbour).astype(jnp.float32))
        dq_parts.append(dq_half)
    dq = jnp.concatenate(dq_parts, axis=-1)
    total = jnp.roll(own_total + jnp.concatenate(arrived_parts, axis=-1), -mf, axis=2)
    grad_keys = total[0].astype(jnp.bfloat16).reshape(rows, width_cells, frames, channels)
    grad_values = total[1].astype(jnp.bfloat16).reshape(rows, width_cells, frames, channels)
    grad_queries = dq.reshape(rows, width_cells, frames, channels)
    return (grad_queries, grad_keys, grad_values)


def solution(mesh):
    spec = P("sy", "groups", None, None)
    return jax.shard_map(
        on_device,
        mesh=mesh,
        in_specs=(spec,) * 6,
        out_specs=(spec,) * 3,
        check_vma=False,
    )
```

```python
import functools

import jax
import jax.numpy as jnp
from jax import lax
from jax.experimental import pallas as pl
from jax.experimental.pallas import tpu as pltpu
from jax.sharding import PartitionSpec as P

HEAD_DIM = 128
TILE = 8
MARGIN = 4


def swap(block, pairs_of):
    n = lax.axis_size("sy")
    route = []
    for i in range(n):
        route.append((i, pairs_of(i, n)))
    return lax.ppermute(block, "sy", route)


def core_partner(i, n):
    return i ^ 1


def chip_neighbour(i, n):
    return (i + 1) % n if i % 2 else (i - 1) % n


def window_pieces(start, span, width):
    if start + span <= width:
        return [(0, start, span)]
    return [(0, start, width - start), (width - start, 0, start + span - width)]


def window_kernel(*refs, nq, nk, tiles, tf, mf):
    q_refs = refs[0:nq]
    do_refs = refs[nq : 2 * nq]
    lse_ref, delta_ref = refs[2 * nq], refs[2 * nq + 1]
    k_refs = refs[2 * nq + 2 : 2 * nq + 2 + nk]
    v_refs = refs[2 * nq + 2 + nk : 2 * nq + 2 + 2 * nk]
    dq_refs = refs[2 * nq + 2 + 2 * nk : 3 * nq + 2 + 2 * nk]
    targets = refs[3 * nq + 2 + 2 * nk :]
    scaling = HEAD_DIM ** (-0.5)
    rows = q_refs[0].shape[0]
    width = targets[0].shape[2]
    span = tf + 2 * mf
    for target in targets:
        target[...] = jnp.zeros_like(target)

    def window(refs_list, pieces):
        parts = []
        for ref in refs_list:
            slabs = [ref[:, dst : dst + size, :] for _, dst, size in pieces]
            parts.append(slabs[0] if len(slabs) == 1 else jnp.concatenate(slabs, axis=1))
        joined = parts[0] if len(parts) == 1 else jnp.concatenate(parts, axis=0)
        return joined.reshape(len(refs_list) * rows * span, HEAD_DIM)

    def query_rows(refs_list, b):
        parts = [ref[:, b * tf : (b + 1) * tf, :].reshape(rows * tf, HEAD_DIM) for ref in refs_list]
        return parts[0] if len(parts) == 1 else jnp.concatenate(parts, axis=0)

    for b in range(tiles):
        pieces = window_pieces(b * tf, span, width)
        kw = window(k_refs, pieces)
        vw = window(v_refs, pieces)
        qb = query_rows(q_refs, b)
        dob = query_rows(do_refs, b)
        nt = (((1,), (1,)), ((), ()))
        scores = lax.dot_general(kw, qb, nt, preferred_element_type=jnp.float32) * scaling
        attention = jnp.exp(scores - lse_ref[b])
        grad_attention = lax.dot_general(vw, dob, nt, preferred_element_type=jnp.float32)
        grad_scores = (attention * (grad_attention - delta_ref[b])).astype(jnp.bfloat16)
        grad_v = jnp.dot(attention.astype(jnp.bfloat16), dob, preferred_element_type=jnp.float32)
        grad_k = jnp.dot(grad_scores, qb, preferred_element_type=jnp.float32) * scaling
        grad_q = jnp.dot(grad_scores.T, kw, preferred_element_type=jnp.float32) * scaling
        grad_q = grad_q.reshape(nq, rows, tf, HEAD_DIM)
        for source, dq_ref in enumerate(dq_refs):
            dq_ref[:, b * tf : (b + 1) * tf, :] = grad_q[source].astype(dq_ref.dtype)
        grad_k = grad_k.reshape(nk, rows, span, HEAD_DIM)
        grad_v = grad_v.reshape(nk, rows, span, HEAD_DIM)
        for block, target in enumerate(targets):
            for src, dst, size in pieces:
                target[0, :, dst : dst + size, :] += grad_k[block, :, src : src + size, :]
                target[1, :, dst : dst + size, :] += grad_v[block, :, src : src + size, :]


def window_pass(queries, grads, stats, keys, values, tiles, tf, mf):
    _, rows, width, channels = queries[0][0].shape
    heads = channels // HEAD_DIM
    nq, nk = len(queries), len(keys)
    kernel = functools.partial(window_kernel, nq=nq, nk=nk, tiles=tiles, tf=tf, mf=mf)

    def member_spec(member):
        return pl.BlockSpec((None, rows, width, HEAD_DIM), lambda h: (member, 0, 0, h))

    def stats_spec(member):
        return pl.BlockSpec((None, None, tiles, 1, nq * rows * tf), lambda h: (member, h, 0, 0, 0))

    qspec = pl.BlockSpec((rows, width, HEAD_DIM), lambda h: (0, 0, h))
    pspec = pl.BlockSpec((2, rows, width, HEAD_DIM), lambda h: (0, 0, 0, h))
    pairs = tiles * nq * rows * tf * nk * rows * (tf + 2 * mf) * heads
    cost = pl.CostEstimate(
        flops=10 * pairs * HEAD_DIM,
        transcendentals=pairs,
        bytes_accessed=(2 * (2 * nq + 2 * nk) + 4 * nq + 8 * nk) * rows * width * channels,
    )
    part = jax.ShapeDtypeStruct((2, rows, width, channels), jnp.float32)
    dq_shape = jax.ShapeDtypeStruct((rows, width, channels), jnp.float32)
    members = list(queries) + list(grads)
    blocks = list(keys) + list(values)
    operands = [arr for arr, _ in members] + [stats, stats] + [arr for arr, _ in blocks]
    in_specs = (
        [member_spec(m) for _, m in members]
        + [stats_spec(0), stats_spec(1)]
        + [member_spec(m) for _, m in blocks]
    )
    return pl.pallas_call(
        kernel,
        grid=(heads,),
        in_specs=in_specs,
        out_specs=[qspec] * nq + [pspec] * nk,
        out_shape=[dq_shape] * nq + [part] * nk,
        cost_estimate=cost,
    )(*operands)


def stats_tiles(stats, tiles, tf):
    rows, width, heads = stats.shape
    tiled = stats.reshape(rows, tiles, tf, heads)
    tiled = jnp.transpose(tiled, (3, 1, 0, 2))
    return tiled.reshape(heads, tiles, 1, rows * tf)


def on_device(queries, key_vecs, value_vecs, outputs_fwd, grad_out, log_norm):
    rows, width_cells, frames, channels = queries.shape
    heads = log_norm.shape[3]
    width = width_cells * frames
    tiles = width_cells // TILE
    tf = TILE * frames
    mf = MARGIN * frames

    qd = jnp.stack([queries.reshape(rows, width, channels), grad_out.reshape(rows, width, channels)])
    row_delta = jnp.einsum(
        "rwhd,rwhd->rwh",
        grad_out.reshape(rows, width, heads, HEAD_DIM),
        outputs_fwd.reshape(rows, width, heads, HEAD_DIM),
        preferred_element_type=jnp.float32,
    )
    stats = jnp.stack(
        [stats_tiles(log_norm.reshape(rows, width, heads), tiles, tf), stats_tiles(row_delta, tiles, tf)]
    )
    kv_own = jnp.stack(
        [
            jnp.roll(key_vecs.reshape(rows, width, channels), mf, axis=1),
            jnp.roll(value_vecs.reshape(rows, width, channels), mf, axis=1),
        ]
    )
    kv_cross = swap(kv_own, chip_neighbour)
    kv_partner = swap(kv_own, core_partner)
    qd_partner = swap(qd, core_partner)
    stats_partner = swap(stats, core_partner)

    dq_local, part_own, part_partner = window_pass(
        [(qd, 0)], [(qd, 1)], stats,
        [(kv_own, 0), (kv_partner, 0)], [(kv_own, 1), (kv_partner, 1)], tiles, tf, mf,
    )
    back_partner = swap(part_partner, core_partner)
    stats_pair = jnp.concatenate([stats, stats_partner], axis=-1)
    dq_mine, dq_theirs, part_cross = window_pass(
        [(qd, 0), (qd_partner, 0)], [(qd, 1), (qd_partner, 1)], stats_pair,
        [(kv_cross, 0)], [(kv_cross, 1)], tiles, tf, mf,
    )
    arrived = swap(part_cross.astype(jnp.bfloat16), chip_neighbour)
    dq_back = swap(dq_theirs, core_partner)
    dq = (dq_local + dq_mine + dq_back).astype(jnp.bfloat16)
    total = jnp.roll(part_own + back_partner + arrived.astype(jnp.float32), -mf, axis=2)
    grad_keys = total[0].astype(jnp.bfloat16).reshape(rows, width_cells, frames, channels)
    grad_values = total[1].astype(jnp.bfloat16).reshape(rows, width_cells, frames, channels)
    grad_queries = dq.reshape(rows, width_cells, frames, channels)
    return (grad_queries, grad_keys, grad_values)


def solution(mesh):
    spec = P("sy", "groups", None, None)
    return jax.shard_map(
        on_device,
        mesh=mesh,
        in_specs=(spec,) * 6,
        out_specs=(spec,) * 3,
        check_vma=False,
    )
```

```python
import functools

import jax
import jax.numpy as jnp
from jax import lax
from jax.experimental import pallas as pl
from jax.experimental.pallas import tpu as pltpu
from jax.sharding import PartitionSpec as P

HEAD_DIM = 128
TILE = 8
MARGIN = 4


def swap(block, pairs_of):
    n = lax.axis_size("sy")
    route = []
    for i in range(n):
        route.append((i, pairs_of(i, n)))
    return lax.ppermute(block, "sy", route)


def core_partner(i, n):
    return i ^ 1


def chip_neighbour(i, n):
    return (i + 1) % n if i % 2 else (i - 1) % n


def window_pieces(start, span, width):
    if start + span <= width:
        return [(0, start, span)]
    return [(0, start, width - start), (width - start, 0, start + span - width)]


def window_kernel(*refs, nq, nk, tiles, tf, mf, narrow):
    q_refs = refs[0:nq]
    do_refs = refs[nq : 2 * nq]
    lse_ref, delta_ref = refs[2 * nq], refs[2 * nq + 1]
    k_refs = refs[2 * nq + 2 : 2 * nq + 2 + nk]
    v_refs = refs[2 * nq + 2 + nk : 2 * nq + 2 + 2 * nk]
    dq_refs = refs[2 * nq + 2 + 2 * nk : 3 * nq + 2 + 2 * nk]
    outs = refs[3 * nq + 2 + 2 * nk : 3 * nq + 2 + 2 * nk + nk]
    targets = refs[3 * nq + 2 + 2 * nk + nk :] if narrow else outs
    scaling = HEAD_DIM ** (-0.5)
    rows = q_refs[0].shape[0]
    width = targets[0].shape[2]
    span = tf + 2 * mf
    for target in targets:
        target[...] = jnp.zeros_like(target)

    def window(refs_list, pieces):
        parts = []
        for ref in refs_list:
            slabs = [ref[:, dst : dst + size, :] for _, dst, size in pieces]
            parts.append(slabs[0] if len(slabs) == 1 else jnp.concatenate(slabs, axis=1))
        joined = parts[0] if len(parts) == 1 else jnp.concatenate(parts, axis=0)
        return joined.reshape(len(refs_list) * rows * span, HEAD_DIM)

    def query_rows(refs_list, b):
        parts = [ref[:, b * tf : (b + 1) * tf, :].reshape(rows * tf, HEAD_DIM) for ref in refs_list]
        return parts[0] if len(parts) == 1 else jnp.concatenate(parts, axis=0)

    for b in range(tiles):
        pieces = window_pieces(b * tf, span, width)
        kw = window(k_refs, pieces)
        vw = window(v_refs, pieces)
        qb = query_rows(q_refs, b)
        dob = query_rows(do_refs, b)
        nt = (((1,), (1,)), ((), ()))
        scores = lax.dot_general(kw, qb, nt, preferred_element_type=jnp.float32) * scaling
        attention = jnp.exp(scores - lse_ref[b])
        grad_attention = lax.dot_general(vw, dob, nt, preferred_element_type=jnp.float32)
        grad_scores = (attention * (grad_attention - delta_ref[b])).astype(jnp.bfloat16)
        grad_v = jnp.dot(attention.astype(jnp.bfloat16), dob, preferred_element_type=jnp.float32)
        grad_k = jnp.dot(grad_scores, qb, preferred_element_type=jnp.float32) * scaling
        grad_q = jnp.dot(grad_scores.T, kw, preferred_element_type=jnp.float32) * scaling
        grad_q = grad_q.reshape(nq, rows, tf, HEAD_DIM)
        for source, dq_ref in enumerate(dq_refs):
            dq_ref[:, b * tf : (b + 1) * tf, :] = grad_q[source].astype(dq_ref.dtype)
        grad_k = grad_k.reshape(nk, rows, span, HEAD_DIM)
        grad_v = grad_v.reshape(nk, rows, span, HEAD_DIM)
        for block, target in enumerate(targets):
            for src, dst, size in pieces:
                target[0, :, dst : dst + size, :] += grad_k[block, :, src : src + size, :]
                target[1, :, dst : dst + size, :] += grad_v[block, :, src : src + size, :]
    if narrow:
        for out, target in zip(outs, targets):
            out[...] = target[...].astype(out.dtype)


def window_pass(queries, grads, stats, keys, values, tiles, tf, mf, first=0, heads=None, narrow=False):
    _, rows, width, all_channels = queries[0][0].shape
    if heads is None:
        heads = all_channels // HEAD_DIM
    channels = heads * HEAD_DIM
    nq, nk = len(queries), len(keys)
    kernel = functools.partial(window_kernel, nq=nq, nk=nk, tiles=tiles, tf=tf, mf=mf, narrow=narrow)

    def member_spec(member):
        return pl.BlockSpec((None, rows, width, HEAD_DIM), lambda h: (member, 0, 0, h + first))

    def stats_spec(member):
        return pl.BlockSpec(
            (None, None, tiles, 1, nq * rows * tf), lambda h: (member, h + first, 0, 0, 0)
        )

    qspec = pl.BlockSpec((rows, width, HEAD_DIM), lambda h: (0, 0, h))
    pspec = pl.BlockSpec((2, rows, width, HEAD_DIM), lambda h: (0, 0, 0, h))
    pairs = tiles * nq * rows * tf * nk * rows * (tf + 2 * mf) * heads
    cost = pl.CostEstimate(
        flops=10 * pairs * HEAD_DIM,
        transcendentals=pairs,
        bytes_accessed=(2 * (2 * nq + 2 * nk) + 4 * nq + 8 * nk) * rows * width * channels,
    )
    part = jax.ShapeDtypeStruct((2, rows, width, channels), jnp.bfloat16 if narrow else jnp.float32)
    scratch = [pltpu.VMEM((2, rows, width, HEAD_DIM), jnp.float32)] * nk if narrow else []
    dq_shape = jax.ShapeDtypeStruct((rows, width, channels), jnp.float32)
    members = list(queries) + list(grads)
    blocks = list(keys) + list(values)
    operands = [arr for arr, _ in members] + [stats, stats] + [arr for arr, _ in blocks]
    in_specs = (
        [member_spec(m) for _, m in members]
        + [stats_spec(0), stats_spec(1)]
        + [member_spec(m) for _, m in blocks]
    )
    return pl.pallas_call(
        kernel,
        grid=(heads,),
        in_specs=in_specs,
        out_specs=[qspec] * nq + [pspec] * nk,
        out_shape=[dq_shape] * nq + [part] * nk,
        scratch_shapes=scratch,
        cost_estimate=cost,
    )(*operands)


def stats_tiles(stats, tiles, tf):
    rows, width, heads = stats.shape
    tiled = stats.reshape(rows, tiles, tf, heads)
    tiled = jnp.transpose(tiled, (3, 1, 0, 2))
    return tiled.reshape(heads, tiles, 1, rows * tf)


def on_device(queries, key_vecs, value_vecs, outputs_fwd, grad_out, log_norm):
    rows, width_cells, frames, channels = queries.shape
    heads = log_norm.shape[3]
    width = width_cells * frames
    tiles = width_cells // TILE
    tf = TILE * frames
    mf = MARGIN * frames

    qd = jnp.stack([queries.reshape(rows, width, channels), grad_out.reshape(rows, width, channels)])
    row_delta = jnp.einsum(
        "rwhd,rwhd->rwh",
        grad_out.reshape(rows, width, heads, HEAD_DIM),
        outputs_fwd.reshape(rows, width, heads, HEAD_DIM),
        preferred_element_type=jnp.float32,
    )
    stats = jnp.stack(
        [stats_tiles(log_norm.reshape(rows, width, heads), tiles, tf), stats_tiles(row_delta, tiles, tf)]
    )
    kv_own = jnp.stack(
        [
            jnp.roll(key_vecs.reshape(rows, width, channels), mf, axis=1),
            jnp.roll(value_vecs.reshape(rows, width, channels), mf, axis=1),
        ]
    )
    kv_cross = swap(kv_own, chip_neighbour)
    kv_partner = swap(kv_own, core_partner)
    qd_partner = swap(qd, core_partner)
    stats_partner = swap(stats, core_partner)

    dq_local, part_own, part_partner = window_pass(
        [(qd, 0)], [(qd, 1)], stats,
        [(kv_own, 0), (kv_partner, 0)], [(kv_own, 1), (kv_partner, 1)], tiles, tf, mf,
    )
    back_partner = swap(part_partner, core_partner)
    stats_pair = jnp.concatenate([stats, stats_partner], axis=-1)
    halves = 1
    count = heads // halves
    mine_parts, back_parts, arrived_parts = [], [], []
    for half in range(halves):
        dq_mine, dq_theirs, part_cross = window_pass(
            [(qd, 0), (qd_partner, 0)], [(qd, 1), (qd_partner, 1)], stats_pair,
            [(kv_cross, 0)], [(kv_cross, 1)], tiles, tf, mf,
            first=half * count, heads=count, narrow=True,
        )
        arrived_parts.append(swap(part_cross, chip_neighbour))
        back_parts.append(swap(dq_theirs, core_partner))
        mine_parts.append(dq_mine)
    dq_mine = jnp.concatenate(mine_parts, axis=-1)
    dq_back = jnp.concatenate(back_parts, axis=-1)
    arrived = jnp.concatenate(arrived_parts, axis=-1)
    dq = (dq_local + dq_mine + dq_back).astype(jnp.bfloat16)
    total = jnp.roll(part_own + back_partner + arrived.astype(jnp.float32), -mf, axis=2)
    grad_keys = total[0].astype(jnp.bfloat16).reshape(rows, width_cells, frames, channels)
    grad_values = total[1].astype(jnp.bfloat16).reshape(rows, width_cells, frames, channels)
    grad_queries = dq.reshape(rows, width_cells, frames, channels)
    return (grad_queries, grad_keys, grad_values)


def solution(mesh):
    spec = P("sy", "groups", None, None)
    return jax.shard_map(
        on_device,
        mesh=mesh,
        in_specs=(spec,) * 6,
        out_specs=(spec,) * 3,
        check_vma=False,
    )
```

```python
import functools

import jax
import jax.numpy as jnp
from jax import lax
from jax.experimental import pallas as pl
from jax.experimental.pallas import tpu as pltpu
from jax.sharding import PartitionSpec as P

HEAD_DIM = 128
TILE = 8
MARGIN = 4


def swap(block, pairs_of):
    n = lax.axis_size("sy")
    route = []
    for i in range(n):
        route.append((i, pairs_of(i, n)))
    return lax.ppermute(block, "sy", route)


def core_partner(i, n):
    return i ^ 1


def chip_neighbour(i, n):
    return (i + 1) % n if i % 2 else (i - 1) % n


def window_pieces(start, span, width):
    if start + span <= width:
        return [(0, start, span)]
    return [(0, start, width - start), (width - start, 0, start + span - width)]


def window_kernel(*refs, nq, nk, tiles, tf, mf, narrow):
    q_refs = refs[0:nq]
    do_refs = refs[nq : 2 * nq]
    lse_ref, delta_ref = refs[2 * nq], refs[2 * nq + 1]
    k_refs = refs[2 * nq + 2 : 2 * nq + 2 + nk]
    v_refs = refs[2 * nq + 2 + nk : 2 * nq + 2 + 2 * nk]
    dq_refs = refs[2 * nq + 2 + 2 * nk : 3 * nq + 2 + 2 * nk]
    outs = refs[3 * nq + 2 + 2 * nk : 3 * nq + 2 + 2 * nk + nk]
    targets = refs[3 * nq + 2 + 2 * nk + nk :] if narrow else outs
    scaling = HEAD_DIM ** (-0.5)
    rows = q_refs[0].shape[0]
    width = targets[0].shape[2]
    span = tf + 2 * mf
    for target in targets:
        target[...] = jnp.zeros_like(target)

    def window(refs_list, pieces):
        parts = []
        for ref in refs_list:
            slabs = [ref[:, dst : dst + size, :] for _, dst, size in pieces]
            parts.append(slabs[0] if len(slabs) == 1 else jnp.concatenate(slabs, axis=1))
        joined = parts[0] if len(parts) == 1 else jnp.concatenate(parts, axis=0)
        return joined.reshape(len(refs_list) * rows * span, HEAD_DIM)

    def query_rows(refs_list, b):
        parts = [ref[:, b * tf : (b + 1) * tf, :].reshape(rows * tf, HEAD_DIM) for ref in refs_list]
        return parts[0] if len(parts) == 1 else jnp.concatenate(parts, axis=0)

    for b in range(tiles):
        pieces = window_pieces(b * tf, span, width)
        kw = window(k_refs, pieces)
        vw = window(v_refs, pieces)
        qb = query_rows(q_refs, b)
        dob = query_rows(do_refs, b)
        nt = (((1,), (1,)), ((), ()))
        scores = lax.dot_general(kw, qb, nt, preferred_element_type=jnp.float32) * scaling
        attention = jnp.exp(scores - lse_ref[b])
        grad_attention = lax.dot_general(vw, dob, nt, preferred_element_type=jnp.float32)
        grad_scores = (attention * (grad_attention - delta_ref[b])).astype(jnp.bfloat16)
        grad_v = jnp.dot(attention.astype(jnp.bfloat16), dob, preferred_element_type=jnp.float32)
        grad_k = jnp.dot(grad_scores, qb, preferred_element_type=jnp.float32) * scaling
        grad_q = jnp.dot(grad_scores.T, kw, preferred_element_type=jnp.float32) * scaling
        grad_q = grad_q.reshape(nq, rows, tf, HEAD_DIM)
        for source, dq_ref in enumerate(dq_refs):
            dq_ref[:, b * tf : (b + 1) * tf, :] = grad_q[source].astype(dq_ref.dtype)
        grad_k = grad_k.reshape(nk, rows, span, HEAD_DIM)
        grad_v = grad_v.reshape(nk, rows, span, HEAD_DIM)
        for block, target in enumerate(targets):
            for src, dst, size in pieces:
                target[0, :, dst : dst + size, :] += grad_k[block, :, src : src + size, :]
                target[1, :, dst : dst + size, :] += grad_v[block, :, src : src + size, :]
    if narrow:
        for out, target in zip(outs, targets):
            out[...] = target[...].astype(out.dtype)


def window_pass(queries, grads, stats, keys, values, tiles, tf, mf, first=0, heads=None, narrow=False):
    _, rows, width, all_channels = queries[0][0].shape
    if heads is None:
        heads = all_channels // HEAD_DIM
    channels = heads * HEAD_DIM
    nq, nk = len(queries), len(keys)
    kernel = functools.partial(window_kernel, nq=nq, nk=nk, tiles=tiles, tf=tf, mf=mf, narrow=narrow)

    def member_spec(member):
        return pl.BlockSpec((None, rows, width, HEAD_DIM), lambda h: (member, 0, 0, h + first))

    def stats_spec(member):
        return pl.BlockSpec(
            (None, None, tiles, 1, nq * rows * tf), lambda h: (member, h + first, 0, 0, 0)
        )

    qspec = pl.BlockSpec((rows, width, HEAD_DIM), lambda h: (0, 0, h))
    pspec = pl.BlockSpec((2, rows, width, HEAD_DIM), lambda h: (0, 0, 0, h))
    pairs = tiles * nq * rows * tf * nk * rows * (tf + 2 * mf) * heads
    cost = pl.CostEstimate(
        flops=10 * pairs * HEAD_DIM,
        transcendentals=pairs,
        bytes_accessed=(2 * (2 * nq + 2 * nk) + 4 * nq + 8 * nk) * rows * width * channels,
    )
    part = jax.ShapeDtypeStruct((2, rows, width, channels), jnp.bfloat16 if narrow else jnp.float32)
    scratch = [pltpu.VMEM((2, rows, width, HEAD_DIM), jnp.float32)] * nk if narrow else []
    dq_shape = jax.ShapeDtypeStruct((rows, width, channels), jnp.float32)
    members = list(queries) + list(grads)
    blocks = list(keys) + list(values)
    operands = [arr for arr, _ in members] + [stats, stats] + [arr for arr, _ in blocks]
    in_specs = (
        [member_spec(m) for _, m in members]
        + [stats_spec(0), stats_spec(1)]
        + [member_spec(m) for _, m in blocks]
    )
    return pl.pallas_call(
        kernel,
        grid=(heads,),
        in_specs=in_specs,
        out_specs=[qspec] * nq + [pspec] * nk,
        out_shape=[dq_shape] * nq + [part] * nk,
        scratch_shapes=scratch,
        cost_estimate=cost,
    )(*operands)


def stats_tiles(stats, tiles, tf):
    rows, width, heads = stats.shape
    tiled = stats.reshape(rows, tiles, tf, heads)
    tiled = jnp.transpose(tiled, (3, 1, 0, 2))
    return tiled.reshape(heads, tiles, 1, rows * tf)


def on_device(queries, key_vecs, value_vecs, outputs_fwd, grad_out, log_norm):
    rows, width_cells, frames, channels = queries.shape
    heads = log_norm.shape[3]
    width = width_cells * frames
    tiles = width_cells // TILE
    tf = TILE * frames
    mf = MARGIN * frames

    qd = jnp.stack([queries.reshape(rows, width, channels), grad_out.reshape(rows, width, channels)])
    row_delta = jnp.einsum(
        "rwhd,rwhd->rwh",
        grad_out.reshape(rows, width, heads, HEAD_DIM),
        outputs_fwd.reshape(rows, width, heads, HEAD_DIM),
        preferred_element_type=jnp.float32,
    )
    stats = jnp.stack(
        [stats_tiles(log_norm.reshape(rows, width, heads), tiles, tf), stats_tiles(row_delta, tiles, tf)]
    )
    kv_own = jnp.stack(
        [
            jnp.roll(key_vecs, MARGIN, axis=1).reshape(rows, width, channels),
            jnp.roll(value_vecs, MARGIN, axis=1).reshape(rows, width, channels),
        ]
    )
    kv_cross = swap(kv_own, chip_neighbour)
    kv_partner = swap(kv_own, core_partner)
    qd_partner = swap(qd, core_partner)
    stats_partner = swap(stats, core_partner)

    dq_local, part_own, part_partner = window_pass(
        [(qd, 0)], [(qd, 1)], stats,
        [(kv_own, 0), (kv_partner, 0)], [(kv_own, 1), (kv_partner, 1)], tiles, tf, mf,
    )
    back_partner = swap(part_partner, core_partner)
    stats_pair = jnp.concatenate([stats, stats_partner], axis=-1)
    halves = 1
    count = heads // halves
    mine_parts, back_parts, arrived_parts = [], [], []
    for half in range(halves):
        dq_mine, dq_theirs, part_cross = window_pass(
            [(qd, 0), (qd_partner, 0)], [(qd, 1), (qd_partner, 1)], stats_pair,
            [(kv_cross, 0)], [(kv_cross, 1)], tiles, tf, mf,
            first=half * count, heads=count, narrow=True,
        )
        arrived_parts.append(swap(part_cross, chip_neighbour))
        back_parts.append(swap(dq_theirs, core_partner))
        mine_parts.append(dq_mine)
    dq_mine = jnp.concatenate(mine_parts, axis=-1)
    dq_back = jnp.concatenate(back_parts, axis=-1)
    arrived = jnp.concatenate(arrived_parts, axis=-1)
    dq = (dq_local + dq_mine + dq_back).astype(jnp.bfloat16)
    total = (part_own + back_partner + arrived.astype(jnp.float32)).astype(jnp.bfloat16)
    grad_keys = jnp.roll(total[0].reshape(rows, width_cells, frames, channels), -MARGIN, axis=1)
    grad_values = jnp.roll(total[1].reshape(rows, width_cells, frames, channels), -MARGIN, axis=1)
    grad_queries = dq.reshape(rows, width_cells, frames, channels)
    return (grad_queries, grad_keys, grad_values)


def solution(mesh):
    spec = P("sy", "groups", None, None)
    return jax.shard_map(
        on_device,
        mesh=mesh,
        in_specs=(spec,) * 6,
        out_specs=(spec,) * 3,
        check_vma=False,
    )
```

```python
import functools

import jax
import jax.numpy as jnp
from jax import lax
from jax.experimental import pallas as pl
from jax.experimental.pallas import tpu as pltpu
from jax.sharding import PartitionSpec as P

HEAD_DIM = 128
TILE = 8
MARGIN = 4


def swap(block, pairs_of):
    n = lax.axis_size("sy")
    route = []
    for i in range(n):
        route.append((i, pairs_of(i, n)))
    return lax.ppermute(block, "sy", route)


def core_partner(i, n):
    return i ^ 1


def chip_neighbour(i, n):
    return (i + 1) % n if i % 2 else (i - 1) % n


def window_pieces(start, span, width):
    if start + span <= width:
        return [(0, start, span)]
    return [(0, start, width - start), (width - start, 0, start + span - width)]


def window_kernel(*refs, nq, nk, tiles, tf, mf, narrow, group):
    q_refs = refs[0:nq]
    do_refs = refs[nq : 2 * nq]
    lse_ref, delta_ref = refs[2 * nq], refs[2 * nq + 1]
    k_refs = refs[2 * nq + 2 : 2 * nq + 2 + nk]
    v_refs = refs[2 * nq + 2 + nk : 2 * nq + 2 + 2 * nk]
    dq_refs = refs[2 * nq + 2 + 2 * nk : 3 * nq + 2 + 2 * nk]
    outs = refs[3 * nq + 2 + 2 * nk : 3 * nq + 2 + 2 * nk + nk]
    targets = refs[3 * nq + 2 + 2 * nk + nk :] if narrow else outs
    scaling = HEAD_DIM ** (-0.5)
    rows = q_refs[0].shape[0]
    width = targets[0].shape[2]
    span = tf + 2 * mf
    for target in targets:
        target[...] = jnp.zeros_like(target)

    def window(refs_list, pieces):
        parts = []
        for ref in refs_list:
            slabs = [ref[:, dst : dst + size, :] for _, dst, size in pieces]
            parts.append(slabs[0] if len(slabs) == 1 else jnp.concatenate(slabs, axis=1))
        joined = parts[0] if len(parts) == 1 else jnp.concatenate(parts, axis=0)
        return joined.reshape(len(refs_list) * rows * span, HEAD_DIM)

    def query_rows(refs_list, b):
        parts = [ref[:, b * tf : (b + 1) * tf, :].reshape(rows * tf, HEAD_DIM) for ref in refs_list]
        return parts[0] if len(parts) == 1 else jnp.concatenate(parts, axis=0)

    for j, b in [(j, b) for j in range(group) for b in range(tiles)]:
        lanes = slice(j * HEAD_DIM, (j + 1) * HEAD_DIM)
        pieces = window_pieces(b * tf, span, width)
        kw = window([ref.at[:, :, lanes] for ref in k_refs], pieces)
        vw = window([ref.at[:, :, lanes] for ref in v_refs], pieces)
        qb = query_rows([ref.at[:, :, lanes] for ref in q_refs], b)
        dob = query_rows([ref.at[:, :, lanes] for ref in do_refs], b)
        nt = (((1,), (1,)), ((), ()))
        scores = lax.dot_general(kw, qb, nt, preferred_element_type=jnp.float32) * scaling
        attention = jnp.exp(scores - lse_ref[j, b])
        grad_attention = lax.dot_general(vw, dob, nt, preferred_element_type=jnp.float32)
        grad_scores = (attention * (grad_attention - delta_ref[j, b])).astype(jnp.bfloat16)
        grad_v = jnp.dot(attention.astype(jnp.bfloat16), dob, preferred_element_type=jnp.float32)
        grad_k = jnp.dot(grad_scores, qb, preferred_element_type=jnp.float32) * scaling
        grad_q = jnp.dot(grad_scores.T, kw, preferred_element_type=jnp.float32) * scaling
        grad_q = grad_q.reshape(nq, rows, tf, HEAD_DIM)
        for source, dq_ref in enumerate(dq_refs):
            dq_ref[:, b * tf : (b + 1) * tf, lanes] = grad_q[source].astype(dq_ref.dtype)
        grad_k = grad_k.reshape(nk, rows, span, HEAD_DIM)
        grad_v = grad_v.reshape(nk, rows, span, HEAD_DIM)
        for block, target in enumerate(targets):
            for src, dst, size in pieces:
                target[0, :, dst : dst + size, lanes] += grad_k[block, :, src : src + size, :]
                target[1, :, dst : dst + size, lanes] += grad_v[block, :, src : src + size, :]
    if narrow:
        for out, target in zip(outs, targets):
            out[...] = target[...].astype(out.dtype)


def window_pass(queries, grads, stats, keys, values, tiles, tf, mf, first=0, heads=None, narrow=False):
    _, rows, width, all_channels = queries[0][0].shape
    if heads is None:
        heads = all_channels // HEAD_DIM
    channels = heads * HEAD_DIM
    nq, nk = len(queries), len(keys)
    group = 2 if heads % 2 == 0 else 1
    kernel = functools.partial(
        window_kernel, nq=nq, nk=nk, tiles=tiles, tf=tf, mf=mf, narrow=narrow, group=group
    )
    lanes = group * HEAD_DIM

    def member_spec(member):
        return pl.BlockSpec((None, rows, width, lanes), lambda h: (member, 0, 0, h + first // group))

    def stats_spec(member):
        return pl.BlockSpec(
            (None, group, tiles, 1, nq * rows * tf), lambda h: (member, h + first // group, 0, 0, 0)
        )

    qspec = pl.BlockSpec((rows, width, lanes), lambda h: (0, 0, h))
    pspec = pl.BlockSpec((2, rows, width, lanes), lambda h: (0, 0, 0, h))
    pairs = tiles * nq * rows * tf * nk * rows * (tf + 2 * mf) * heads
    cost = pl.CostEstimate(
        flops=10 * pairs * HEAD_DIM,
        transcendentals=pairs,
        bytes_accessed=(2 * (2 * nq + 2 * nk) + 4 * nq + 8 * nk) * rows * width * channels,
    )
    part = jax.ShapeDtypeStruct((2, rows, width, channels), jnp.bfloat16 if narrow else jnp.float32)
    scratch = [pltpu.VMEM((2, rows, width, lanes), jnp.float32)] * nk if narrow else []
    dq_shape = jax.ShapeDtypeStruct((rows, width, channels), jnp.float32)
    members = list(queries) + list(grads)
    blocks = list(keys) + list(values)
    operands = [arr for arr, _ in members] + [stats, stats] + [arr for arr, _ in blocks]
    in_specs = (
        [member_spec(m) for _, m in members]
        + [stats_spec(0), stats_spec(1)]
        + [member_spec(m) for _, m in blocks]
    )
    return pl.pallas_call(
        kernel,
        grid=(heads // group,),
        in_specs=in_specs,
        out_specs=[qspec] * nq + [pspec] * nk,
        out_shape=[dq_shape] * nq + [part] * nk,
        scratch_shapes=scratch,
        cost_estimate=cost,
    )(*operands)


def stats_tiles(stats, tiles, tf):
    rows, width, heads = stats.shape
    tiled = stats.reshape(rows, tiles, tf, heads)
    tiled = jnp.transpose(tiled, (3, 1, 0, 2))
    return tiled.reshape(heads, tiles, 1, rows * tf)


def on_device(queries, key_vecs, value_vecs, outputs_fwd, grad_out, log_norm):
    rows, width_cells, frames, channels = queries.shape
    heads = log_norm.shape[3]
    width = width_cells * frames
    tiles = width_cells // TILE
    tf = TILE * frames
    mf = MARGIN * frames

    qd = jnp.stack([queries.reshape(rows, width, channels), grad_out.reshape(rows, width, channels)])
    row_delta = jnp.einsum(
        "rwhd,rwhd->rwh",
        grad_out.reshape(rows, width, heads, HEAD_DIM),
        outputs_fwd.reshape(rows, width, heads, HEAD_DIM),
        preferred_element_type=jnp.float32,
    )
    stats = jnp.stack(
        [stats_tiles(log_norm.reshape(rows, width, heads), tiles, tf), stats_tiles(row_delta, tiles, tf)]
    )
    kv_own = jnp.stack(
        [
            jnp.roll(key_vecs.reshape(rows, width, channels), mf, axis=1),
            jnp.roll(value_vecs.reshape(rows, width, channels), mf, axis=1),
        ]
    )
    kv_cross = swap(kv_own, chip_neighbour)
    kv_partner = swap(kv_own, core_partner)
    qd_partner = swap(qd, core_partner)
    stats_partner = swap(stats, core_partner)

    dq_local, part_own, part_partner = window_pass(
        [(qd, 0)], [(qd, 1)], stats,
        [(kv_own, 0), (kv_partner, 0)], [(kv_own, 1), (kv_partner, 1)], tiles, tf, mf,
    )
    back_partner = swap(part_partner, core_partner)
    stats_pair = jnp.concatenate([stats, stats_partner], axis=-1)
    halves = 1
    count = heads // halves
    mine_parts, back_parts, arrived_parts = [], [], []
    for half in range(halves):
        dq_mine, dq_theirs, part_cross = window_pass(
            [(qd, 0), (qd_partner, 0)], [(qd, 1), (qd_partner, 1)], stats_pair,
            [(kv_cross, 0)], [(kv_cross, 1)], tiles, tf, mf,
            first=half * count, heads=count, narrow=True,
        )
        arrived_parts.append(swap(part_cross, chip_neighbour))
        back_parts.append(swap(dq_theirs, core_partner))
        mine_parts.append(dq_mine)
    dq_mine = jnp.concatenate(mine_parts, axis=-1)
    dq_back = jnp.concatenate(back_parts, axis=-1)
    arrived = jnp.concatenate(arrived_parts, axis=-1)
    dq = (dq_local + dq_mine + dq_back).astype(jnp.bfloat16)
    total = jnp.roll(part_own + back_partner + arrived.astype(jnp.float32), -mf, axis=2)
    grad_keys = total[0].astype(jnp.bfloat16).reshape(rows, width_cells, frames, channels)
    grad_values = total[1].astype(jnp.bfloat16).reshape(rows, width_cells, frames, channels)
    grad_queries = dq.reshape(rows, width_cells, frames, channels)
    return (grad_queries, grad_keys, grad_values)


def solution(mesh):
    spec = P("sy", "groups", None, None)
    return jax.shard_map(
        on_device,
        mesh=mesh,
        in_specs=(spec,) * 6,
        out_specs=(spec,) * 3,
        check_vma=False,
    )
```

```python
import functools

import jax
import jax.numpy as jnp
from jax import lax
from jax.experimental import pallas as pl
from jax.experimental.pallas import tpu as pltpu
from jax.sharding import PartitionSpec as P

HEAD_DIM = 128
TILE = 8
MARGIN = 4


def swap(block, pairs_of):
    n = lax.axis_size("sy")
    route = []
    for i in range(n):
        route.append((i, pairs_of(i, n)))
    return lax.ppermute(block, "sy", route)


def core_partner(i, n):
    return i ^ 1


def chip_neighbour(i, n):
    return (i + 1) % n if i % 2 else (i - 1) % n


def window_pieces(start, span, width):
    if start + span <= width:
        return [(0, start, span)]
    return [(0, start, width - start), (width - start, 0, start + span - width)]


def window_kernel(*refs, nq, nk, tiles, tf, mf, narrow, group):
    q_refs = refs[0:nq]
    do_refs = refs[nq : 2 * nq]
    lse_ref, delta_ref = refs[2 * nq], refs[2 * nq + 1]
    k_refs = refs[2 * nq + 2 : 2 * nq + 2 + nk]
    v_refs = refs[2 * nq + 2 + nk : 2 * nq + 2 + 2 * nk]
    dq_refs = refs[2 * nq + 2 + 2 * nk : 3 * nq + 2 + 2 * nk]
    outs = refs[3 * nq + 2 + 2 * nk : 3 * nq + 2 + 2 * nk + nk]
    targets = refs[3 * nq + 2 + 2 * nk + nk :] if narrow else outs
    scaling = HEAD_DIM ** (-0.5)
    rows = q_refs[0].shape[0]
    width = targets[0].shape[2]
    span = tf + 2 * mf
    for target in targets:
        target[...] = jnp.zeros_like(target)

    def window(refs_list, pieces):
        parts = []
        for ref in refs_list:
            slabs = [ref[:, dst : dst + size, :] for _, dst, size in pieces]
            parts.append(slabs[0] if len(slabs) == 1 else jnp.concatenate(slabs, axis=1))
        joined = parts[0] if len(parts) == 1 else jnp.concatenate(parts, axis=0)
        return joined.reshape(len(refs_list) * rows * span, HEAD_DIM)

    def query_rows(refs_list, b):
        parts = [ref[:, b * tf : (b + 1) * tf, :].reshape(rows * tf, HEAD_DIM) for ref in refs_list]
        return parts[0] if len(parts) == 1 else jnp.concatenate(parts, axis=0)

    for j, b in [(j, b) for j in range(group) for b in range(tiles)]:
        lanes = slice(j * HEAD_DIM, (j + 1) * HEAD_DIM)
        pieces = window_pieces(b * tf, span, width)
        kw = window([ref.at[:, :, lanes] for ref in k_refs], pieces)
        vw = window([ref.at[:, :, lanes] for ref in v_refs], pieces)
        qb = query_rows([ref.at[:, :, lanes] for ref in q_refs], b)
        dob = query_rows([ref.at[:, :, lanes] for ref in do_refs], b)
        nt = (((1,), (1,)), ((), ()))
        scores = lax.dot_general(kw, qb, nt, preferred_element_type=jnp.float32) * scaling
        attention = jnp.exp(scores - lse_ref[j, b])
        grad_attention = lax.dot_general(vw, dob, nt, preferred_element_type=jnp.float32)
        grad_scores = (attention * (grad_attention - delta_ref[j, b])).astype(jnp.bfloat16)
        grad_v = jnp.dot(attention.astype(jnp.bfloat16), dob, preferred_element_type=jnp.float32)
        grad_k = jnp.dot(grad_scores, qb, preferred_element_type=jnp.float32) * scaling
        grad_q = jnp.dot(grad_scores.T, kw, preferred_element_type=jnp.float32) * scaling
        grad_q = grad_q.reshape(nq, rows, tf, HEAD_DIM)
        for source, dq_ref in enumerate(dq_refs):
            dq_ref[:, b * tf : (b + 1) * tf, lanes] = grad_q[source].astype(dq_ref.dtype)
        grad_k = grad_k.reshape(nk, rows, span, HEAD_DIM)
        grad_v = grad_v.reshape(nk, rows, span, HEAD_DIM)
        for block, target in enumerate(targets):
            for src, dst, size in pieces:
                target[0, :, dst : dst + size, lanes] += grad_k[block, :, src : src + size, :]
                target[1, :, dst : dst + size, lanes] += grad_v[block, :, src : src + size, :]
    if narrow:
        for out, target in zip(outs, targets):
            out[...] = target[...].astype(out.dtype)


def window_pass(queries, grads, stats, keys, values, tiles, tf, mf, first=0, heads=None, narrow=False):
    _, rows, width, all_channels = queries[0][0].shape
    if heads is None:
        heads = all_channels // HEAD_DIM
    channels = heads * HEAD_DIM
    nq, nk = len(queries), len(keys)
    group = 4 if heads % 4 == 0 else (2 if heads % 2 == 0 else 1)
    kernel = functools.partial(
        window_kernel, nq=nq, nk=nk, tiles=tiles, tf=tf, mf=mf, narrow=narrow, group=group
    )
    lanes = group * HEAD_DIM

    def member_spec(member):
        return pl.BlockSpec((None, rows, width, lanes), lambda h: (member, 0, 0, h + first // group))

    def stats_spec(member):
        return pl.BlockSpec(
            (None, group, tiles, 1, nq * rows * tf), lambda h: (member, h + first // group, 0, 0, 0)
        )

    qspec = pl.BlockSpec((rows, width, lanes), lambda h: (0, 0, h))
    pspec = pl.BlockSpec((2, rows, width, lanes), lambda h: (0, 0, 0, h))
    pairs = tiles * nq * rows * tf * nk * rows * (tf + 2 * mf) * heads
    cost = pl.CostEstimate(
        flops=10 * pairs * HEAD_DIM,
        transcendentals=pairs,
        bytes_accessed=(2 * (2 * nq + 2 * nk) + 4 * nq + 8 * nk) * rows * width * channels,
    )
    part = jax.ShapeDtypeStruct((2, rows, width, channels), jnp.bfloat16 if narrow else jnp.float32)
    scratch = [pltpu.VMEM((2, rows, width, lanes), jnp.float32)] * nk if narrow else []
    dq_shape = jax.ShapeDtypeStruct((rows, width, channels), jnp.float32)
    members = list(queries) + list(grads)
    blocks = list(keys) + list(values)
    operands = [arr for arr, _ in members] + [stats, stats] + [arr for arr, _ in blocks]
    in_specs = (
        [member_spec(m) for _, m in members]
        + [stats_spec(0), stats_spec(1)]
        + [member_spec(m) for _, m in blocks]
    )
    return pl.pallas_call(
        kernel,
        grid=(heads // group,),
        in_specs=in_specs,
        out_specs=[qspec] * nq + [pspec] * nk,
        out_shape=[dq_shape] * nq + [part] * nk,
        scratch_shapes=scratch,
        cost_estimate=cost,
    )(*operands)


def stats_tiles(stats, tiles, tf):
    rows, width, heads = stats.shape
    tiled = stats.reshape(rows, tiles, tf, heads)
    tiled = jnp.transpose(tiled, (3, 1, 0, 2))
    return tiled.reshape(heads, tiles, 1, rows * tf)


def on_device(queries, key_vecs, value_vecs, outputs_fwd, grad_out, log_norm):
    rows, width_cells, frames, channels = queries.shape
    heads = log_norm.shape[3]
    width = width_cells * frames
    tiles = width_cells // TILE
    tf = TILE * frames
    mf = MARGIN * frames

    qd = jnp.stack([queries.reshape(rows, width, channels), grad_out.reshape(rows, width, channels)])
    row_delta = jnp.einsum(
        "rwhd,rwhd->rwh",
        grad_out.reshape(rows, width, heads, HEAD_DIM),
        outputs_fwd.reshape(rows, width, heads, HEAD_DIM),
        preferred_element_type=jnp.float32,
    )
    stats = jnp.stack(
        [stats_tiles(log_norm.reshape(rows, width, heads), tiles, tf), stats_tiles(row_delta, tiles, tf)]
    )
    kv_own = jnp.stack(
        [
            jnp.roll(key_vecs.reshape(rows, width, channels), mf, axis=1),
            jnp.roll(value_vecs.reshape(rows, width, channels), mf, axis=1),
        ]
    )
    kv_cross = swap(kv_own, chip_neighbour)
    kv_partner = swap(kv_own, core_partner)
    qd_partner = swap(qd, core_partner)
    stats_partner = swap(stats, core_partner)

    dq_local, part_own, part_partner = window_pass(
        [(qd, 0)], [(qd, 1)], stats,
        [(kv_own, 0), (kv_partner, 0)], [(kv_own, 1), (kv_partner, 1)], tiles, tf, mf,
    )
    back_partner = swap(part_partner, core_partner)
    stats_pair = jnp.concatenate([stats, stats_partner], axis=-1)
    halves = 1
    count = heads // halves
    mine_parts, back_parts, arrived_parts = [], [], []
    for half in range(halves):
        dq_mine, dq_theirs, part_cross = window_pass(
            [(qd, 0), (qd_partner, 0)], [(qd, 1), (qd_partner, 1)], stats_pair,
            [(kv_cross, 0)], [(kv_cross, 1)], tiles, tf, mf,
            first=half * count, heads=count, narrow=True,
        )
        arrived_parts.append(swap(part_cross, chip_neighbour))
        back_parts.append(swap(dq_theirs, core_partner))
        mine_parts.append(dq_mine)
    dq_mine = jnp.concatenate(mine_parts, axis=-1)
    dq_back = jnp.concatenate(back_parts, axis=-1)
    arrived = jnp.concatenate(arrived_parts, axis=-1)
    dq = (dq_local + dq_mine + dq_back).astype(jnp.bfloat16)
    total = jnp.roll(part_own + back_partner + arrived.astype(jnp.float32), -mf, axis=2)
    grad_keys = total[0].astype(jnp.bfloat16).reshape(rows, width_cells, frames, channels)
    grad_values = total[1].astype(jnp.bfloat16).reshape(rows, width_cells, frames, channels)
    grad_queries = dq.reshape(rows, width_cells, frames, channels)
    return (grad_queries, grad_keys, grad_values)


def solution(mesh):
    spec = P("sy", "groups", None, None)
    return jax.shard_map(
        on_device,
        mesh=mesh,
        in_specs=(spec,) * 6,
        out_specs=(spec,) * 3,
        check_vma=False,
    )
```

```python
import functools

import jax
import jax.numpy as jnp
from jax import lax
from jax.experimental import pallas as pl
from jax.experimental.pallas import tpu as pltpu
from jax.sharding import PartitionSpec as P

HEAD_DIM = 128
TILE = 8
MARGIN = 4


def swap(block, pairs_of):
    n = lax.axis_size("sy")
    route = []
    for i in range(n):
        route.append((i, pairs_of(i, n)))
    return lax.ppermute(block, "sy", route)


def core_partner(i, n):
    return i ^ 1


def chip_neighbour(i, n):
    return (i + 1) % n if i % 2 else (i - 1) % n


def window_pieces(start, span, width):
    if start + span <= width:
        return [(0, start, span)]
    return [(0, start, width - start), (width - start, 0, start + span - width)]


def window_kernel(*refs, nq, nk, tiles, tf, mf, narrow, group):
    q_refs = refs[0:nq]
    do_refs = refs[nq : 2 * nq]
    lse_ref, delta_ref = refs[2 * nq], refs[2 * nq + 1]
    k_refs = refs[2 * nq + 2 : 2 * nq + 2 + nk]
    v_refs = refs[2 * nq + 2 + nk : 2 * nq + 2 + 2 * nk]
    dq_refs = refs[2 * nq + 2 + 2 * nk : 3 * nq + 2 + 2 * nk]
    outs = refs[3 * nq + 2 + 2 * nk : 3 * nq + 2 + 2 * nk + nk]
    targets = refs[3 * nq + 2 + 2 * nk + nk :] if narrow else outs
    scaling = HEAD_DIM ** (-0.5)
    rows = q_refs[0].shape[0]
    width = targets[0].shape[2]
    span = tf + 2 * mf
    for target in targets:
        target[...] = jnp.zeros_like(target)

    def window(refs_list, pieces):
        parts = []
        for ref in refs_list:
            slabs = [ref[:, dst : dst + size, :] for _, dst, size in pieces]
            parts.append(slabs[0] if len(slabs) == 1 else jnp.concatenate(slabs, axis=1))
        joined = parts[0] if len(parts) == 1 else jnp.concatenate(parts, axis=0)
        return joined.reshape(len(refs_list) * rows * span, HEAD_DIM)

    def query_rows(refs_list, b):
        parts = [ref[:, b * tf : (b + 1) * tf, :].reshape(rows * tf, HEAD_DIM) for ref in refs_list]
        return parts[0] if len(parts) == 1 else jnp.concatenate(parts, axis=0)

    for j, b in [(j, b) for j in range(group) for b in range(tiles)]:
        lanes = slice(j * HEAD_DIM, (j + 1) * HEAD_DIM)
        pieces = window_pieces(b * tf, span, width)
        kw = window([ref.at[:, :, lanes] for ref in k_refs], pieces)
        vw = window([ref.at[:, :, lanes] for ref in v_refs], pieces)
        qb = query_rows([ref.at[:, :, lanes] for ref in q_refs], b)
        dob = query_rows([ref.at[:, :, lanes] for ref in do_refs], b)
        nt = (((1,), (1,)), ((), ()))
        scores = lax.dot_general(kw, qb, nt, preferred_element_type=jnp.float32) * scaling
        attention = jnp.exp(scores - lse_ref[j, b])
        grad_attention = lax.dot_general(vw, dob, nt, preferred_element_type=jnp.float32)
        grad_scores = (attention * (grad_attention - delta_ref[j, b])).astype(jnp.bfloat16)
        grad_v = jnp.dot(attention.astype(jnp.bfloat16), dob, preferred_element_type=jnp.float32)
        grad_k = jnp.dot(grad_scores, qb, preferred_element_type=jnp.float32) * scaling
        grad_q = jnp.dot(grad_scores.T, kw, preferred_element_type=jnp.float32) * scaling
        grad_q = grad_q.reshape(nq, rows, tf, HEAD_DIM)
        for source, dq_ref in enumerate(dq_refs):
            dq_ref[:, b * tf : (b + 1) * tf, lanes] = grad_q[source].astype(dq_ref.dtype)
        grad_k = grad_k.reshape(nk, rows, span, HEAD_DIM)
        grad_v = grad_v.reshape(nk, rows, span, HEAD_DIM)
        stores = window_pieces((b * tf - mf) % width, span, width)
        for block, target in enumerate(targets):
            for src, dst, size in stores:
                target[0, :, dst : dst + size, lanes] += grad_k[block, :, src : src + size, :]
                target[1, :, dst : dst + size, lanes] += grad_v[block, :, src : src + size, :]
    if narrow:
        for out, target in zip(outs, targets):
            out[...] = target[...].astype(out.dtype)


def window_pass(queries, grads, stats, keys, values, tiles, tf, mf, first=0, heads=None, narrow=False):
    _, rows, width, all_channels = queries[0][0].shape
    if heads is None:
        heads = all_channels // HEAD_DIM
    channels = heads * HEAD_DIM
    nq, nk = len(queries), len(keys)
    group = 4 if heads % 4 == 0 else (2 if heads % 2 == 0 else 1)
    kernel = functools.partial(
        window_kernel, nq=nq, nk=nk, tiles=tiles, tf=tf, mf=mf, narrow=narrow, group=group
    )
    lanes = group * HEAD_DIM

    def member_spec(member):
        return pl.BlockSpec((None, rows, width, lanes), lambda h: (member, 0, 0, h + first // group))

    def stats_spec(member):
        return pl.BlockSpec(
            (None, group, tiles, 1, nq * rows * tf), lambda h: (member, h + first // group, 0, 0, 0)
        )

    qspec = pl.BlockSpec((rows, width, lanes), lambda h: (0, 0, h))
    pspec = pl.BlockSpec((2, rows, width, lanes), lambda h: (0, 0, 0, h))
    pairs = tiles * nq * rows * tf * nk * rows * (tf + 2 * mf) * heads
    cost = pl.CostEstimate(
        flops=10 * pairs * HEAD_DIM,
        transcendentals=pairs,
        bytes_accessed=(2 * (2 * nq + 2 * nk) + 4 * nq + 8 * nk) * rows * width * channels,
    )
    part = jax.ShapeDtypeStruct((2, rows, width, channels), jnp.bfloat16 if narrow else jnp.float32)
    scratch = [pltpu.VMEM((2, rows, width, lanes), jnp.float32)] * nk if narrow else []
    dq_shape = jax.ShapeDtypeStruct((rows, width, channels), jnp.float32)
    members = list(queries) + list(grads)
    blocks = list(keys) + list(values)
    operands = [arr for arr, _ in members] + [stats, stats] + [arr for arr, _ in blocks]
    in_specs = (
        [member_spec(m) for _, m in members]
        + [stats_spec(0), stats_spec(1)]
        + [member_spec(m) for _, m in blocks]
    )
    return pl.pallas_call(
        kernel,
        grid=(heads // group,),
        in_specs=in_specs,
        out_specs=[qspec] * nq + [pspec] * nk,
        out_shape=[dq_shape] * nq + [part] * nk,
        scratch_shapes=scratch,
        cost_estimate=cost,
    )(*operands)


def stats_tiles(stats, tiles, tf):
    rows, width, heads = stats.shape
    tiled = stats.reshape(rows, tiles, tf, heads)
    tiled = jnp.transpose(tiled, (3, 1, 0, 2))
    return tiled.reshape(heads, tiles, 1, rows * tf)


def on_device(queries, key_vecs, value_vecs, outputs_fwd, grad_out, log_norm):
    rows, width_cells, frames, channels = queries.shape
    heads = log_norm.shape[3]
    width = width_cells * frames
    tiles = width_cells // TILE
    tf = TILE * frames
    mf = MARGIN * frames

    qd = jnp.stack([queries.reshape(rows, width, channels), grad_out.reshape(rows, width, channels)])
    row_delta = jnp.einsum(
        "rwhd,rwhd->rwh",
        grad_out.reshape(rows, width, heads, HEAD_DIM),
        outputs_fwd.reshape(rows, width, heads, HEAD_DIM),
        preferred_element_type=jnp.float32,
    )
    stats = jnp.stack(
        [stats_tiles(log_norm.reshape(rows, width, heads), tiles, tf), stats_tiles(row_delta, tiles, tf)]
    )
    kv_own = jnp.stack(
        [
            jnp.roll(key_vecs.reshape(rows, width, channels), mf, axis=1),
            jnp.roll(value_vecs.reshape(rows, width, channels), mf, axis=1),
        ]
    )
    kv_cross = swap(kv_own, chip_neighbour)
    kv_partner = swap(kv_own, core_partner)
    qd_partner = swap(qd, core_partner)
    stats_partner = swap(stats, core_partner)

    dq_local, part_own, part_partner = window_pass(
        [(qd, 0)], [(qd, 1)], stats,
        [(kv_own, 0), (kv_partner, 0)], [(kv_own, 1), (kv_partner, 1)], tiles, tf, mf,
    )
    back_partner = swap(part_partner, core_partner)
    stats_pair = jnp.concatenate([stats, stats_partner], axis=-1)
    halves = 1
    count = heads // halves
    mine_parts, back_parts, arrived_parts = [], [], []
    for half in range(halves):
        dq_mine, dq_theirs, part_cross = window_pass(
            [(qd, 0), (qd_partner, 0)], [(qd, 1), (qd_partner, 1)], stats_pair,
            [(kv_cross, 0)], [(kv_cross, 1)], tiles, tf, mf,
            first=half * count, heads=count, narrow=True,
        )
        arrived_parts.append(swap(part_cross, chip_neighbour))
        back_parts.append(swap(dq_theirs, core_partner))
        mine_parts.append(dq_mine)
    dq_mine = jnp.concatenate(mine_parts, axis=-1)
    dq_back = jnp.concatenate(back_parts, axis=-1)
    arrived = jnp.concatenate(arrived_parts, axis=-1)
    dq = (dq_local + dq_mine + dq_back).astype(jnp.bfloat16)
    total = part_own + back_partner + arrived.astype(jnp.float32)
    grad_keys = total[0].astype(jnp.bfloat16).reshape(rows, width_cells, frames, channels)
    grad_values = total[1].astype(jnp.bfloat16).reshape(rows, width_cells, frames, channels)
    grad_queries = dq.reshape(rows, width_cells, frames, channels)
    return (grad_queries, grad_keys, grad_values)


def solution(mesh):
    spec = P("sy", "groups", None, None)
    return jax.shard_map(
        on_device,
        mesh=mesh,
        in_specs=(spec,) * 6,
        out_specs=(spec,) * 3,
        check_vma=False,
    )
```

```python
import functools

import jax
import jax.numpy as jnp
from jax import lax
from jax.experimental import pallas as pl
from jax.experimental.pallas import tpu as pltpu
from jax.sharding import PartitionSpec as P

HEAD_DIM = 128
TILE = 8
MARGIN = 4


def swap(block, pairs_of):
    n = lax.axis_size("sy")
    route = []
    for i in range(n):
        route.append((i, pairs_of(i, n)))
    return lax.ppermute(block, "sy", route)


def core_partner(i, n):
    return i ^ 1


def chip_neighbour(i, n):
    return (i + 1) % n if i % 2 else (i - 1) % n


def window_pieces(start, span, width):
    if start + span <= width:
        return [(0, start, span)]
    return [(0, start, width - start), (width - start, 0, start + span - width)]


def window_kernel(*refs, nq, nk, tiles, tf, mf, narrow, group):
    q_refs = refs[0:nq]
    do_refs = refs[nq : 2 * nq]
    lse_ref, delta_ref = refs[2 * nq], refs[2 * nq + 1]
    k_refs = refs[2 * nq + 2 : 2 * nq + 2 + nk]
    v_refs = refs[2 * nq + 2 + nk : 2 * nq + 2 + 2 * nk]
    dq_refs = refs[2 * nq + 2 + 2 * nk : 3 * nq + 2 + 2 * nk]
    outs = refs[3 * nq + 2 + 2 * nk : 3 * nq + 2 + 2 * nk + nk]
    targets = refs[3 * nq + 2 + 2 * nk + nk :] if narrow else outs
    scaling = HEAD_DIM ** (-0.5)
    rows = q_refs[0].shape[0]
    width = targets[0].shape[2]
    span = tf + 2 * mf
    for target in targets:
        target[...] = jnp.zeros_like(target)

    def window(refs_list, pieces):
        parts = []
        for ref in refs_list:
            slabs = [ref[:, dst : dst + size, :] for _, dst, size in pieces]
            parts.append(slabs[0] if len(slabs) == 1 else jnp.concatenate(slabs, axis=1))
        joined = parts[0] if len(parts) == 1 else jnp.concatenate(parts, axis=0)
        return joined.reshape(len(refs_list) * rows * span, HEAD_DIM)

    def query_rows(refs_list, b):
        parts = [ref[:, b * tf : (b + 1) * tf, :].reshape(rows * tf, HEAD_DIM) for ref in refs_list]
        return parts[0] if len(parts) == 1 else jnp.concatenate(parts, axis=0)

    for j, b in [(j, b) for j in range(group) for b in range(tiles)]:
        lanes = slice(j * HEAD_DIM, (j + 1) * HEAD_DIM)
        pieces = window_pieces((b * tf - mf) % width, span, width)
        kw = window([ref.at[:, :, lanes] for ref in k_refs], pieces)
        vw = window([ref.at[:, :, lanes] for ref in v_refs], pieces)
        qb = query_rows([ref.at[:, :, lanes] for ref in q_refs], b)
        dob = query_rows([ref.at[:, :, lanes] for ref in do_refs], b)
        nt = (((1,), (1,)), ((), ()))
        scores = lax.dot_general(kw, qb, nt, preferred_element_type=jnp.float32) * scaling
        attention = jnp.exp(scores - lse_ref[j, b])
        grad_attention = lax.dot_general(vw, dob, nt, preferred_element_type=jnp.float32)
        grad_scores = (attention * (grad_attention - delta_ref[j, b])).astype(jnp.bfloat16)
        grad_v = jnp.dot(attention.astype(jnp.bfloat16), dob, preferred_element_type=jnp.float32)
        grad_k = jnp.dot(grad_scores, qb, preferred_element_type=jnp.float32) * scaling
        grad_q = jnp.dot(grad_scores.T, kw, preferred_element_type=jnp.float32) * scaling
        grad_q = grad_q.reshape(nq, rows, tf, HEAD_DIM)
        for source, dq_ref in enumerate(dq_refs):
            dq_ref[:, b * tf : (b + 1) * tf, lanes] = grad_q[source].astype(dq_ref.dtype)
        grad_k = grad_k.reshape(nk, rows, span, HEAD_DIM)
        grad_v = grad_v.reshape(nk, rows, span, HEAD_DIM)
        stores = window_pieces((b * tf - mf) % width, span, width)
        for block, target in enumerate(targets):
            for src, dst, size in stores:
                target[0, :, dst : dst + size, lanes] += grad_k[block, :, src : src + size, :]
                target[1, :, dst : dst + size, lanes] += grad_v[block, :, src : src + size, :]
    if narrow:
        for out, target in zip(outs, targets):
            out[...] = target[...].astype(out.dtype)


def window_pass(queries, grads, stats, keys, values, tiles, tf, mf, first=0, heads=None, narrow=False):
    _, rows, width, all_channels = queries[0][0].shape
    if heads is None:
        heads = all_channels // HEAD_DIM
    channels = heads * HEAD_DIM
    nq, nk = len(queries), len(keys)
    group = 4 if heads % 4 == 0 else (2 if heads % 2 == 0 else 1)
    kernel = functools.partial(
        window_kernel, nq=nq, nk=nk, tiles=tiles, tf=tf, mf=mf, narrow=narrow, group=group
    )
    lanes = group * HEAD_DIM

    def member_spec(member):
        return pl.BlockSpec((None, rows, width, lanes), lambda h: (member, 0, 0, h + first // group))

    def stats_spec(member):
        return pl.BlockSpec(
            (None, group, tiles, 1, nq * rows * tf), lambda h: (member, h + first // group, 0, 0, 0)
        )

    qspec = pl.BlockSpec((rows, width, lanes), lambda h: (0, 0, h))
    pspec = pl.BlockSpec((2, rows, width, lanes), lambda h: (0, 0, 0, h))
    pairs = tiles * nq * rows * tf * nk * rows * (tf + 2 * mf) * heads
    cost = pl.CostEstimate(
        flops=10 * pairs * HEAD_DIM,
        transcendentals=pairs,
        bytes_accessed=(2 * (2 * nq + 2 * nk) + 4 * nq + 8 * nk) * rows * width * channels,
    )
    part = jax.ShapeDtypeStruct((2, rows, width, channels), jnp.bfloat16 if narrow else jnp.float32)
    scratch = [pltpu.VMEM((2, rows, width, lanes), jnp.float32)] * nk if narrow else []
    dq_shape = jax.ShapeDtypeStruct((rows, width, channels), jnp.float32)
    members = list(queries) + list(grads)
    blocks = list(keys) + list(values)
    operands = [arr for arr, _ in members] + [stats, stats] + [arr for arr, _ in blocks]
    in_specs = (
        [member_spec(m) for _, m in members]
        + [stats_spec(0), stats_spec(1)]
        + [member_spec(m) for _, m in blocks]
    )
    return pl.pallas_call(
        kernel,
        grid=(heads // group,),
        in_specs=in_specs,
        out_specs=[qspec] * nq + [pspec] * nk,
        out_shape=[dq_shape] * nq + [part] * nk,
        scratch_shapes=scratch,
        cost_estimate=cost,
    )(*operands)


def stats_tiles(stats, tiles, tf):
    rows, width, heads = stats.shape
    tiled = stats.reshape(rows, tiles, tf, heads)
    tiled = jnp.transpose(tiled, (3, 1, 0, 2))
    return tiled.reshape(heads, tiles, 1, rows * tf)


def on_device(queries, key_vecs, value_vecs, outputs_fwd, grad_out, log_norm):
    rows, width_cells, frames, channels = queries.shape
    heads = log_norm.shape[3]
    width = width_cells * frames
    tiles = width_cells // TILE
    tf = TILE * frames
    mf = MARGIN * frames

    qd = jnp.stack([queries.reshape(rows, width, channels), grad_out.reshape(rows, width, channels)])
    row_delta = jnp.einsum(
        "rwhd,rwhd->rwh",
        grad_out.reshape(rows, width, heads, HEAD_DIM),
        outputs_fwd.reshape(rows, width, heads, HEAD_DIM),
        preferred_element_type=jnp.float32,
    )
    stats = jnp.stack(
        [stats_tiles(log_norm.reshape(rows, width, heads), tiles, tf), stats_tiles(row_delta, tiles, tf)]
    )
    kv_own = jnp.stack(
        [
            key_vecs.reshape(rows, width, channels),
            value_vecs.reshape(rows, width, channels),
        ]
    )
    kv_cross = swap(kv_own, chip_neighbour)
    kv_partner = swap(kv_own, core_partner)
    qd_partner = swap(qd, core_partner)
    stats_partner = swap(stats, core_partner)

    dq_local, part_own, part_partner = window_pass(
        [(qd, 0)], [(qd, 1)], stats,
        [(kv_own, 0), (kv_partner, 0)], [(kv_own, 1), (kv_partner, 1)], tiles, tf, mf,
    )
    back_partner = swap(part_partner, core_partner)
    stats_pair = jnp.concatenate([stats, stats_partner], axis=-1)
    halves = 1
    count = heads // halves
    mine_parts, back_parts, arrived_parts = [], [], []
    for half in range(halves):
        dq_mine, dq_theirs, part_cross = window_pass(
            [(qd, 0), (qd_partner, 0)], [(qd, 1), (qd_partner, 1)], stats_pair,
            [(kv_cross, 0)], [(kv_cross, 1)], tiles, tf, mf,
            first=half * count, heads=count, narrow=True,
        )
        arrived_parts.append(swap(part_cross, chip_neighbour))
        back_parts.append(swap(dq_theirs, core_partner))
        mine_parts.append(dq_mine)
    dq_mine = jnp.concatenate(mine_parts, axis=-1)
    dq_back = jnp.concatenate(back_parts, axis=-1)
    arrived = jnp.concatenate(arrived_parts, axis=-1)
    dq = (dq_local + dq_mine + dq_back).astype(jnp.bfloat16)
    total = part_own + back_partner + arrived.astype(jnp.float32)
    grad_keys = total[0].astype(jnp.bfloat16).reshape(rows, width_cells, frames, channels)
    grad_values = total[1].astype(jnp.bfloat16).reshape(rows, width_cells, frames, channels)
    grad_queries = dq.reshape(rows, width_cells, frames, channels)
    return (grad_queries, grad_keys, grad_values)


def solution(mesh):
    spec = P("sy", "groups", None, None)
    return jax.shard_map(
        on_device,
        mesh=mesh,
        in_specs=(spec,) * 6,
        out_specs=(spec,) * 3,
        check_vma=False,
    )
```

```python
import functools

import jax
import jax.numpy as jnp
from jax import lax
from jax.experimental import pallas as pl
from jax.experimental.pallas import tpu as pltpu
from jax.sharding import PartitionSpec as P

HEAD_DIM = 128
TILE = 8
MARGIN = 4


def swap(block, pairs_of):
    n = lax.axis_size("sy")
    route = []
    for i in range(n):
        route.append((i, pairs_of(i, n)))
    return lax.ppermute(block, "sy", route)


def core_partner(i, n):
    return i ^ 1


def chip_neighbour(i, n):
    return (i + 1) % n if i % 2 else (i - 1) % n


def window_pieces(start, span, width):
    if start + span <= width:
        return [(0, start, span)]
    return [(0, start, width - start), (width - start, 0, start + span - width)]


def window_kernel(*refs, nq, nk, tiles, tf, mf, narrow, group):
    q_refs = refs[0:nq]
    do_refs = refs[nq : 2 * nq]
    lse_ref, delta_ref = refs[2 * nq], refs[2 * nq + 1]
    k_refs = refs[2 * nq + 2 : 2 * nq + 2 + nk]
    v_refs = refs[2 * nq + 2 + nk : 2 * nq + 2 + 2 * nk]
    dq_refs = refs[2 * nq + 2 + 2 * nk : 3 * nq + 2 + 2 * nk]
    outs = refs[3 * nq + 2 + 2 * nk : 3 * nq + 2 + 2 * nk + nk]
    targets = refs[3 * nq + 2 + 2 * nk + nk :] if narrow else outs
    scaling = HEAD_DIM ** (-0.5)
    rows = q_refs[0].shape[0]
    width = targets[0].shape[2]
    span = tf + 2 * mf
    for target in targets:
        target[...] = jnp.zeros_like(target)

    def window(refs_list, pieces):
        parts = []
        for ref in refs_list:
            slabs = [ref[:, dst : dst + size, :] for _, dst, size in pieces]
            parts.append(slabs[0] if len(slabs) == 1 else jnp.concatenate(slabs, axis=1))
        joined = parts[0] if len(parts) == 1 else jnp.concatenate(parts, axis=0)
        return joined.reshape(len(refs_list) * rows * span, HEAD_DIM)

    def query_rows(refs_list, b):
        parts = [ref[:, b * tf : (b + 1) * tf, :].reshape(rows * tf, HEAD_DIM) for ref in refs_list]
        return parts[0] if len(parts) == 1 else jnp.concatenate(parts, axis=0)

    for j, b in [(j, b) for j in range(group) for b in range(tiles)]:
        lanes = slice(j * HEAD_DIM, (j + 1) * HEAD_DIM)
        pieces = window_pieces(b * tf, span, width)
        kw = window([ref.at[:, :, lanes] for ref in k_refs], pieces)
        vw = window([ref.at[:, :, lanes] for ref in v_refs], pieces)
        qb = query_rows([ref.at[:, :, lanes] for ref in q_refs], b)
        dob = query_rows([ref.at[:, :, lanes] for ref in do_refs], b)
        nt = (((1,), (1,)), ((), ()))
        scores = lax.dot_general(kw, qb, nt, preferred_element_type=jnp.float32) * scaling
        attention = jnp.exp(scores - lse_ref[j, b])
        grad_attention = lax.dot_general(vw, dob, nt, preferred_element_type=jnp.float32)
        grad_scores = (attention * (grad_attention - delta_ref[j, b])).astype(jnp.bfloat16)
        grad_v = jnp.dot(attention.astype(jnp.bfloat16), dob, preferred_element_type=jnp.float32)
        grad_k = jnp.dot(grad_scores, qb, preferred_element_type=jnp.float32) * scaling
        grad_q = jnp.dot(grad_scores.T, kw, preferred_element_type=jnp.float32) * scaling
        grad_q = grad_q.reshape(nq, rows, tf, HEAD_DIM)
        for source, dq_ref in enumerate(dq_refs):
            dq_ref[:, b * tf : (b + 1) * tf, lanes] = grad_q[source].astype(dq_ref.dtype)
        grad_k = grad_k.reshape(nk, rows, span, HEAD_DIM)
        grad_v = grad_v.reshape(nk, rows, span, HEAD_DIM)
        stores = window_pieces((b * tf - mf) % width, span, width)
        for block, target in enumerate(targets):
            for src, dst, size in stores:
                target[0, :, dst : dst + size, lanes] += grad_k[block, :, src : src + size, :]
                target[1, :, dst : dst + size, lanes] += grad_v[block, :, src : src + size, :]
    if narrow:
        for out, target in zip(outs, targets):
            out[...] = target[...].astype(out.dtype)


def window_pass(queries, grads, stats, keys, values, tiles, tf, mf, first=0, heads=None, narrow=False):
    _, rows, width, all_channels = queries[0][0].shape
    if heads is None:
        heads = all_channels // HEAD_DIM
    channels = heads * HEAD_DIM
    nq, nk = len(queries), len(keys)
    group = 6 if heads % 6 == 0 else (2 if heads % 2 == 0 else 1)
    kernel = functools.partial(
        window_kernel, nq=nq, nk=nk, tiles=tiles, tf=tf, mf=mf, narrow=narrow, group=group
    )
    lanes = group * HEAD_DIM

    def member_spec(member):
        return pl.BlockSpec((None, rows, width, lanes), lambda h: (member, 0, 0, h + first // group))

    def stats_spec(member):
        return pl.BlockSpec(
            (None, group, tiles, 1, nq * rows * tf), lambda h: (member, h + first // group, 0, 0, 0)
        )

    qspec = pl.BlockSpec((rows, width, lanes), lambda h: (0, 0, h))
    pspec = pl.BlockSpec((2, rows, width, lanes), lambda h: (0, 0, 0, h))
    pairs = tiles * nq * rows * tf * nk * rows * (tf + 2 * mf) * heads
    cost = pl.CostEstimate(
        flops=10 * pairs * HEAD_DIM,
        transcendentals=pairs,
        bytes_accessed=(2 * (2 * nq + 2 * nk) + 4 * nq + 8 * nk) * rows * width * channels,
    )
    part = jax.ShapeDtypeStruct((2, rows, width, channels), jnp.bfloat16 if narrow else jnp.float32)
    scratch = [pltpu.VMEM((2, rows, width, lanes), jnp.float32)] * nk if narrow else []
    dq_shape = jax.ShapeDtypeStruct((rows, width, channels), jnp.float32)
    members = list(queries) + list(grads)
    blocks = list(keys) + list(values)
    operands = [arr for arr, _ in members] + [stats, stats] + [arr for arr, _ in blocks]
    in_specs = (
        [member_spec(m) for _, m in members]
        + [stats_spec(0), stats_spec(1)]
        + [member_spec(m) for _, m in blocks]
    )
    return pl.pallas_call(
        kernel,
        grid=(heads // group,),
        in_specs=in_specs,
        out_specs=[qspec] * nq + [pspec] * nk,
        out_shape=[dq_shape] * nq + [part] * nk,
        scratch_shapes=scratch,
        cost_estimate=cost,
    )(*operands)


def stats_tiles(stats, tiles, tf):
    rows, width, heads = stats.shape
    tiled = stats.reshape(rows, tiles, tf, heads)
    tiled = jnp.transpose(tiled, (3, 1, 0, 2))
    return tiled.reshape(heads, tiles, 1, rows * tf)


def on_device(queries, key_vecs, value_vecs, outputs_fwd, grad_out, log_norm):
    rows, width_cells, frames, channels = queries.shape
    heads = log_norm.shape[3]
    width = width_cells * frames
    tiles = width_cells // TILE
    tf = TILE * frames
    mf = MARGIN * frames

    qd = jnp.stack([queries.reshape(rows, width, channels), grad_out.reshape(rows, width, channels)])
    row_delta = jnp.einsum(
        "rwhd,rwhd->rwh",
        grad_out.reshape(rows, width, heads, HEAD_DIM),
        outputs_fwd.reshape(rows, width, heads, HEAD_DIM),
        preferred_element_type=jnp.float32,
    )
    stats = jnp.stack(
        [stats_tiles(log_norm.reshape(rows, width, heads), tiles, tf), stats_tiles(row_delta, tiles, tf)]
    )
    kv_own = jnp.stack(
        [
            jnp.roll(key_vecs.reshape(rows, width, channels), mf, axis=1),
            jnp.roll(value_vecs.reshape(rows, width, channels), mf, axis=1),
        ]
    )
    kv_cross = swap(kv_own, chip_neighbour)
    kv_partner = swap(kv_own, core_partner)
    qd_partner = swap(qd, core_partner)
    stats_partner = swap(stats, core_partner)

    dq_local, part_own, part_partner = window_pass(
        [(qd, 0)], [(qd, 1)], stats,
        [(kv_own, 0), (kv_partner, 0)], [(kv_own, 1), (kv_partner, 1)], tiles, tf, mf,
    )
    back_partner = swap(part_partner, core_partner)
    stats_pair = jnp.concatenate([stats, stats_partner], axis=-1)
    halves = 1
    count = heads // halves
    mine_parts, back_parts, arrived_parts = [], [], []
    for half in range(halves):
        dq_mine, dq_theirs, part_cross = window_pass(
            [(qd, 0), (qd_partner, 0)], [(qd, 1), (qd_partner, 1)], stats_pair,
            [(kv_cross, 0)], [(kv_cross, 1)], tiles, tf, mf,
            first=half * count, heads=count, narrow=True,
        )
        arrived_parts.append(swap(part_cross, chip_neighbour))
        back_parts.append(swap(dq_theirs, core_partner))
        mine_parts.append(dq_mine)
    dq_mine = jnp.concatenate(mine_parts, axis=-1)
    dq_back = jnp.concatenate(back_parts, axis=-1)
    arrived = jnp.concatenate(arrived_parts, axis=-1)
    dq = (dq_local + dq_mine + dq_back).astype(jnp.bfloat16)
    total = part_own + back_partner + arrived.astype(jnp.float32)
    grad_keys = total[0].astype(jnp.bfloat16).reshape(rows, width_cells, frames, channels)
    grad_values = total[1].astype(jnp.bfloat16).reshape(rows, width_cells, frames, channels)
    grad_queries = dq.reshape(rows, width_cells, frames, channels)
    return (grad_queries, grad_keys, grad_values)


def solution(mesh):
    spec = P("sy", "groups", None, None)
    return jax.shard_map(
        on_device,
        mesh=mesh,
        in_specs=(spec,) * 6,
        out_specs=(spec,) * 3,
        check_vma=False,
    )
```

```python
import functools

import jax
import jax.numpy as jnp
from jax import lax
from jax.experimental import pallas as pl
from jax.experimental.pallas import tpu as pltpu
from jax.sharding import PartitionSpec as P

HEAD_DIM = 128
TILE = 8
MARGIN = 4


def swap(block, pairs_of):
    n = lax.axis_size("sy")
    route = []
    for i in range(n):
        route.append((i, pairs_of(i, n)))
    return lax.ppermute(block, "sy", route)


def core_partner(i, n):
    return i ^ 1


def chip_neighbour(i, n):
    return (i + 1) % n if i % 2 else (i - 1) % n


def window_pieces(start, span, width):
    if start + span <= width:
        return [(0, start, span)]
    return [(0, start, width - start), (width - start, 0, start + span - width)]


def window_kernel(*refs, nq, nk, tiles, tf, mf, narrow, group):
    q_refs = refs[0:nq]
    do_refs = refs[nq : 2 * nq]
    lse_ref, delta_ref = refs[2 * nq], refs[2 * nq + 1]
    k_refs = refs[2 * nq + 2 : 2 * nq + 2 + nk]
    v_refs = refs[2 * nq + 2 + nk : 2 * nq + 2 + 2 * nk]
    dq_refs = refs[2 * nq + 2 + 2 * nk : 3 * nq + 2 + 2 * nk]
    outs = refs[3 * nq + 2 + 2 * nk : 3 * nq + 2 + 2 * nk + nk]
    targets = refs[3 * nq + 2 + 2 * nk + nk :] if narrow else outs
    scaling = HEAD_DIM ** (-0.5)
    rows = q_refs[0].shape[0]
    width = targets[0].shape[2]
    span = tf + 2 * mf
    for target in targets:
        target[...] = jnp.zeros_like(target)

    def window(refs_list, pieces):
        parts = []
        for ref in refs_list:
            slabs = [ref[:, dst : dst + size, :] for _, dst, size in pieces]
            parts.append(slabs[0] if len(slabs) == 1 else jnp.concatenate(slabs, axis=1))
        joined = parts[0] if len(parts) == 1 else jnp.concatenate(parts, axis=0)
        return joined.reshape(len(refs_list) * rows * span, HEAD_DIM)

    def query_rows(refs_list, b):
        parts = [ref[:, b * tf : (b + 1) * tf, :].reshape(rows * tf, HEAD_DIM) for ref in refs_list]
        return parts[0] if len(parts) == 1 else jnp.concatenate(parts, axis=0)

    for j, b in [(j, b) for j in range(group) for b in range(tiles)]:
        lanes = slice(j * HEAD_DIM, (j + 1) * HEAD_DIM)
        pieces = window_pieces(b * tf, span, width)
        kw = window([ref.at[:, :, lanes] for ref in k_refs], pieces)
        vw = window([ref.at[:, :, lanes] for ref in v_refs], pieces)
        qb = query_rows([ref.at[:, :, lanes] for ref in q_refs], b)
        dob = query_rows([ref.at[:, :, lanes] for ref in do_refs], b)
        nt = (((1,), (1,)), ((), ()))
        scores = lax.dot_general(kw, qb, nt, preferred_element_type=jnp.float32) * scaling
        attention = jnp.exp(scores - lse_ref[j, b])
        grad_attention = lax.dot_general(vw, dob, nt, preferred_element_type=jnp.float32)
        grad_scores = (attention * (grad_attention - delta_ref[j, b])).astype(jnp.bfloat16)
        grad_v = jnp.dot(attention.astype(jnp.bfloat16), dob, preferred_element_type=jnp.float32)
        grad_k = jnp.dot(grad_scores, qb, preferred_element_type=jnp.float32) * scaling
        grad_q = jnp.dot(grad_scores.T, kw, preferred_element_type=jnp.float32) * scaling
        grad_q = grad_q.reshape(nq, rows, tf, HEAD_DIM)
        for source, dq_ref in enumerate(dq_refs):
            dq_ref[:, b * tf : (b + 1) * tf, lanes] = grad_q[source].astype(dq_ref.dtype)
        grad_k = grad_k.reshape(nk, rows, span, HEAD_DIM)
        grad_v = grad_v.reshape(nk, rows, span, HEAD_DIM)
        stores = window_pieces((b * tf - mf) % width, span, width)
        for block, target in enumerate(targets):
            for src, dst, size in stores:
                target[0, :, dst : dst + size, lanes] += grad_k[block, :, src : src + size, :]
                target[1, :, dst : dst + size, lanes] += grad_v[block, :, src : src + size, :]
    if narrow:
        for out, target in zip(outs, targets):
            out[...] = target[...].astype(out.dtype)


def window_pass(queries, grads, stats, keys, values, tiles, tf, mf, first=0, heads=None, narrow=False):
    _, rows, width, all_channels = queries[0][0].shape
    if heads is None:
        heads = all_channels // HEAD_DIM
    channels = heads * HEAD_DIM
    nq, nk = len(queries), len(keys)
    group = 4 if heads % 4 == 0 else (2 if heads % 2 == 0 else 1)
    kernel = functools.partial(
        window_kernel, nq=nq, nk=nk, tiles=tiles, tf=tf, mf=mf, narrow=narrow, group=group
    )
    lanes = group * HEAD_DIM

    def member_spec(member):
        return pl.BlockSpec((None, rows, width, lanes), lambda h: (member, 0, 0, h + first // group))

    def stats_spec(member):
        return pl.BlockSpec(
            (None, group, tiles, 1, nq * rows * tf), lambda h: (member, h + first // group, 0, 0, 0)
        )

    qspec = pl.BlockSpec((rows, width, lanes), lambda h: (0, 0, h))
    pspec = pl.BlockSpec((2, rows, width, lanes), lambda h: (0, 0, 0, h))
    pairs = tiles * nq * rows * tf * nk * rows * (tf + 2 * mf) * heads
    cost = pl.CostEstimate(
        flops=10 * pairs * HEAD_DIM,
        transcendentals=pairs,
        bytes_accessed=(2 * (2 * nq + 2 * nk) + 4 * nq + 8 * nk) * rows * width * channels,
    )
    part = jax.ShapeDtypeStruct((2, rows, width, channels), jnp.bfloat16 if narrow else jnp.float32)
    scratch = [pltpu.VMEM((2, rows, width, lanes), jnp.float32)] * nk if narrow else []
    dq_shape = jax.ShapeDtypeStruct((rows, width, channels), jnp.float32)
    members = list(queries) + list(grads)
    blocks = list(keys) + list(values)
    operands = [arr for arr, _ in members] + [stats, stats] + [arr for arr, _ in blocks]
    in_specs = (
        [member_spec(m) for _, m in members]
        + [stats_spec(0), stats_spec(1)]
        + [member_spec(m) for _, m in blocks]
    )
    return pl.pallas_call(
        kernel,
        grid=(heads // group,),
        in_specs=in_specs,
        out_specs=[qspec] * nq + [pspec] * nk,
        out_shape=[dq_shape] * nq + [part] * nk,
        scratch_shapes=scratch,
        cost_estimate=cost,
    )(*operands)


def stats_tiles(stats, tiles, tf):
    rows, width, heads = stats.shape
    tiled = stats.reshape(rows, tiles, tf, heads)
    tiled = jnp.transpose(tiled, (3, 1, 0, 2))
    return tiled.reshape(heads, tiles, 1, rows * tf)


def on_device(queries, key_vecs, value_vecs, outputs_fwd, grad_out, log_norm):
    rows, width_cells, frames, channels = queries.shape
    heads = log_norm.shape[3]
    width = width_cells * frames
    tiles = width_cells // TILE
    tf = TILE * frames
    mf = MARGIN * frames

    qd = jnp.stack([queries.reshape(rows, width, channels), grad_out.reshape(rows, width, channels)])
    row_delta = jnp.einsum(
        "rwhd,rwhd->rwh",
        grad_out.reshape(rows, width, heads, HEAD_DIM),
        outputs_fwd.reshape(rows, width, heads, HEAD_DIM),
        preferred_element_type=jnp.float32,
    )
    stats = jnp.stack(
        [stats_tiles(log_norm.reshape(rows, width, heads), tiles, tf), stats_tiles(row_delta, tiles, tf)]
    )
    kv_own = jnp.stack(
        [
            jnp.roll(key_vecs.reshape(rows, width, channels), mf, axis=1),
            jnp.roll(value_vecs.reshape(rows, width, channels), mf, axis=1),
        ]
    )
    kv_cross = swap(kv_own, chip_neighbour)
    kv_partner = swap(kv_own, core_partner)
    qd_partner = swap(qd, core_partner)
    stats_partner = swap(stats, core_partner)

    dq_local, part_own, part_partner = window_pass(
        [(qd, 0)], [(qd, 1)], stats,
        [(kv_own, 0), (kv_partner, 0)], [(kv_own, 1), (kv_partner, 1)], tiles, tf, mf,
    )
    back_partner = swap(part_partner, core_partner)
    stats_pair = jnp.concatenate([stats, stats_partner], axis=-1)
    halves = 1
    count = heads // halves
    mine_parts, back_parts, arrived_parts = [], [], []
    for half in range(halves):
        dq_mine, dq_theirs, part_cross = window_pass(
            [(qd, 0), (qd_partner, 0)], [(qd, 1), (qd_partner, 1)], stats_pair,
            [(kv_cross, 0)], [(kv_cross, 1)], tiles, tf, mf,
            first=half * count, heads=count, narrow=True,
        )
        arrived_parts.append(swap(part_cross, chip_neighbour))
        back_parts.append(swap(dq_theirs, core_partner))
        mine_parts.append(dq_mine)
    dq_mine = jnp.concatenate(mine_parts, axis=-1)
    dq_back = jnp.concatenate(back_parts, axis=-1)
    arrived = jnp.concatenate(arrived_parts, axis=-1)
    dq = (dq_local + dq_mine + dq_back).astype(jnp.bfloat16)
    def finished(member):
        total = part_own[member] + back_partner[member] + arrived[member].astype(jnp.float32)
        return total.reshape(rows, width_cells, frames, channels).astype(jnp.bfloat16)

    grad_keys = finished(0)
    grad_values = finished(1)
    grad_queries = dq.reshape(rows, width_cells, frames, channels)
    return (grad_queries, grad_keys, grad_values)


def solution(mesh):
    spec = P("sy", "groups", None, None)
    return jax.shard_map(
        on_device,
        mesh=mesh,
        in_specs=(spec,) * 6,
        out_specs=(spec,) * 3,
        check_vma=False,
    )
```

```python
import functools

import jax
import jax.numpy as jnp
from jax import lax
from jax.experimental import pallas as pl
from jax.experimental.pallas import tpu as pltpu
from jax.sharding import PartitionSpec as P

HEAD_DIM = 128
TILE = 8
MARGIN = 4


def swap(block, pairs_of):
    n = lax.axis_size("sy")
    route = []
    for i in range(n):
        route.append((i, pairs_of(i, n)))
    return lax.ppermute(block, "sy", route)


def core_partner(i, n):
    return i ^ 1


def chip_neighbour(i, n):
    return (i + 1) % n if i % 2 else (i - 1) % n


def window_pieces(start, span, width):
    if start + span <= width:
        return [(0, start, span)]
    return [(0, start, width - start), (width - start, 0, start + span - width)]


def window_kernel(*refs, nq, nk, tiles, tf, mf, narrow, group):
    q_refs = refs[0:nq]
    do_refs = refs[nq : 2 * nq]
    lse_ref, delta_ref = refs[2 * nq], refs[2 * nq + 1]
    k_refs = refs[2 * nq + 2 : 2 * nq + 2 + nk]
    v_refs = refs[2 * nq + 2 + nk : 2 * nq + 2 + 2 * nk]
    dq_refs = refs[2 * nq + 2 + 2 * nk : 3 * nq + 2 + 2 * nk]
    outs = refs[3 * nq + 2 + 2 * nk : 3 * nq + 2 + 2 * nk + nk]
    targets = refs[3 * nq + 2 + 2 * nk + nk :] if narrow else outs
    scaling = HEAD_DIM ** (-0.5)
    rows = q_refs[0].shape[0]
    width = targets[0].shape[2]
    span = tf + 2 * mf
    for target in targets:
        target[...] = jnp.zeros_like(target)

    def window(refs_list, pieces):
        parts = []
        for ref in refs_list:
            slabs = [ref[:, dst : dst + size, :] for _, dst, size in pieces]
            parts.append(slabs[0] if len(slabs) == 1 else jnp.concatenate(slabs, axis=1))
        joined = parts[0] if len(parts) == 1 else jnp.concatenate(parts, axis=0)
        return joined.reshape(len(refs_list) * rows * span, HEAD_DIM)

    def query_rows(refs_list, b):
        parts = [ref[:, b * tf : (b + 1) * tf, :].reshape(rows * tf, HEAD_DIM) for ref in refs_list]
        return parts[0] if len(parts) == 1 else jnp.concatenate(parts, axis=0)

    for j, b in [(j, b) for j in range(group) for b in range(tiles)]:
        lanes = slice(j * HEAD_DIM, (j + 1) * HEAD_DIM)
        pieces = window_pieces(b * tf, span, width)
        kw = window([ref.at[:, :, lanes] for ref in k_refs], pieces)
        vw = window([ref.at[:, :, lanes] for ref in v_refs], pieces)
        qb = query_rows([ref.at[:, :, lanes] for ref in q_refs], b)
        dob = query_rows([ref.at[:, :, lanes] for ref in do_refs], b)
        nt = (((1,), (1,)), ((), ()))
        scores = lax.dot_general(kw, qb, nt, preferred_element_type=jnp.float32) * scaling
        attention = jnp.exp(scores - lse_ref[j, b])
        grad_attention = lax.dot_general(vw, dob, nt, preferred_element_type=jnp.float32)
        grad_scores = (attention * (grad_attention - delta_ref[j, b])).astype(jnp.bfloat16)
        grad_v = jnp.dot(attention.astype(jnp.bfloat16), dob, preferred_element_type=jnp.float32)
        grad_k = jnp.dot(grad_scores, qb, preferred_element_type=jnp.float32) * scaling
        grad_q = jnp.dot(grad_scores.T, kw, preferred_element_type=jnp.float32) * scaling
        grad_q = grad_q.reshape(nq, rows, tf, HEAD_DIM)
        for source, dq_ref in enumerate(dq_refs):
            dq_ref[:, b * tf : (b + 1) * tf, lanes] = grad_q[source].astype(dq_ref.dtype)
        grad_k = grad_k.reshape(nk, rows, span, HEAD_DIM)
        grad_v = grad_v.reshape(nk, rows, span, HEAD_DIM)
        stores = window_pieces((b * tf - mf) % width, span, width)
        for block, target in enumerate(targets):
            for src, dst, size in stores:
                target[0, :, dst : dst + size, lanes] += grad_k[block, :, src : src + size, :]
                target[1, :, dst : dst + size, lanes] += grad_v[block, :, src : src + size, :]
    if narrow:
        for out, target in zip(outs, targets):
            out[...] = target[...].astype(out.dtype)


def window_pass(queries, grads, stats, keys, values, tiles, tf, mf, first=0, heads=None, narrow=False):
    _, rows, width, all_channels = queries[0][0].shape
    if heads is None:
        heads = all_channels // HEAD_DIM
    channels = heads * HEAD_DIM
    nq, nk = len(queries), len(keys)
    group = 4 if heads % 4 == 0 else (2 if heads % 2 == 0 else 1)
    if narrow and heads % 6 == 0:
        group = 6
    kernel = functools.partial(
        window_kernel, nq=nq, nk=nk, tiles=tiles, tf=tf, mf=mf, narrow=narrow, group=group
    )
    lanes = group * HEAD_DIM

    def member_spec(member):
        return pl.BlockSpec((None, rows, width, lanes), lambda h: (member, 0, 0, h + first // group))

    def stats_spec(member):
        return pl.BlockSpec(
            (None, group, tiles, 1, nq * rows * tf), lambda h: (member, h + first // group, 0, 0, 0)
        )

    qspec = pl.BlockSpec((rows, width, lanes), lambda h: (0, 0, h))
    pspec = pl.BlockSpec((2, rows, width, lanes), lambda h: (0, 0, 0, h))
    pairs = tiles * nq * rows * tf * nk * rows * (tf + 2 * mf) * heads
    cost = pl.CostEstimate(
        flops=10 * pairs * HEAD_DIM,
        transcendentals=pairs,
        bytes_accessed=(2 * (2 * nq + 2 * nk) + 4 * nq + 8 * nk) * rows * width * channels,
    )
    part = jax.ShapeDtypeStruct((2, rows, width, channels), jnp.bfloat16 if narrow else jnp.float32)
    scratch = [pltpu.VMEM((2, rows, width, lanes), jnp.float32)] * nk if narrow else []
    dq_shape = jax.ShapeDtypeStruct((rows, width, channels), jnp.float32)
    members = list(queries) + list(grads)
    blocks = list(keys) + list(values)
    operands = [arr for arr, _ in members] + [stats, stats] + [arr for arr, _ in blocks]
    in_specs = (
        [member_spec(m) for _, m in members]
        + [stats_spec(0), stats_spec(1)]
        + [member_spec(m) for _, m in blocks]
    )
    return pl.pallas_call(
        kernel,
        grid=(heads // group,),
        in_specs=in_specs,
        out_specs=[qspec] * nq + [pspec] * nk,
        out_shape=[dq_shape] * nq + [part] * nk,
        scratch_shapes=scratch,
        cost_estimate=cost,
    )(*operands)


def stats_tiles(stats, tiles, tf):
    rows, width, heads = stats.shape
    tiled = stats.reshape(rows, tiles, tf, heads)
    tiled = jnp.transpose(tiled, (3, 1, 0, 2))
    return tiled.reshape(heads, tiles, 1, rows * tf)


def on_device(queries, key_vecs, value_vecs, outputs_fwd, grad_out, log_norm):
    rows, width_cells, frames, channels = queries.shape
    heads = log_norm.shape[3]
    width = width_cells * frames
    tiles = width_cells // TILE
    tf = TILE * frames
    mf = MARGIN * frames

    qd = jnp.stack([queries.reshape(rows, width, channels), grad_out.reshape(rows, width, channels)])
    row_delta = jnp.einsum(
        "rwhd,rwhd->rwh",
        grad_out.reshape(rows, width, heads, HEAD_DIM),
        outputs_fwd.reshape(rows, width, heads, HEAD_DIM),
        preferred_element_type=jnp.float32,
    )
    stats = jnp.stack(
        [stats_tiles(log_norm.reshape(rows, width, heads), tiles, tf), stats_tiles(row_delta, tiles, tf)]
    )
    kv_own = jnp.stack(
        [
            jnp.roll(key_vecs.reshape(rows, width, channels), mf, axis=1),
            jnp.roll(value_vecs.reshape(rows, width, channels), mf, axis=1),
        ]
    )
    kv_cross = swap(kv_own, chip_neighbour)
    kv_partner = swap(kv_own, core_partner)
    qd_partner = swap(qd, core_partner)
    stats_partner = swap(stats, core_partner)

    dq_local, part_own, part_partner = window_pass(
        [(qd, 0)], [(qd, 1)], stats,
        [(kv_own, 0), (kv_partner, 0)], [(kv_own, 1), (kv_partner, 1)], tiles, tf, mf,
    )
    back_partner = swap(part_partner, core_partner)
    stats_pair = jnp.concatenate([stats, stats_partner], axis=-1)
    halves = 1
    count = heads // halves
    mine_parts, back_parts, arrived_parts = [], [], []
    for half in range(halves):
        dq_mine, dq_theirs, part_cross = window_pass(
            [(qd, 0), (qd_partner, 0)], [(qd, 1), (qd_partner, 1)], stats_pair,
            [(kv_cross, 0)], [(kv_cross, 1)], tiles, tf, mf,
            first=half * count, heads=count, narrow=True,
        )
        arrived_parts.append(swap(part_cross, chip_neighbour))
        back_parts.append(swap(dq_theirs, core_partner))
        mine_parts.append(dq_mine)
    dq_mine = jnp.concatenate(mine_parts, axis=-1)
    dq_back = jnp.concatenate(back_parts, axis=-1)
    arrived = jnp.concatenate(arrived_parts, axis=-1)
    dq = (dq_local + dq_mine + dq_back).astype(jnp.bfloat16)
    total = part_own + back_partner + arrived.astype(jnp.float32)
    grad_keys = total[0].astype(jnp.bfloat16).reshape(rows, width_cells, frames, channels)
    grad_values = total[1].astype(jnp.bfloat16).reshape(rows, width_cells, frames, channels)
    grad_queries = dq.reshape(rows, width_cells, frames, channels)
    return (grad_queries, grad_keys, grad_values)


def solution(mesh):
    spec = P("sy", "groups", None, None)
    return jax.shard_map(
        on_device,
        mesh=mesh,
        in_specs=(spec,) * 6,
        out_specs=(spec,) * 3,
        check_vma=False,
    )
```
